512 devices in a mesh: req: 128 (over x, z, core), mlp: 4 (over y).
Axes of the slice: x: 4, y: 4, z: 16, core: 2. Of those that a mesh axis runs over, the one named last changes fastest.
Arguments:
- queries: bfloat16 [32768, 8, 256], P('req', 'mlp'), may hold values from -7 to 7
- new_kv: bfloat16 [32768, 8, 512], P('req', 'mlp'), may hold values from -6 to 6
- cache_pool: bfloat16 [768, 128, 8, 512], P('req', None, 'mlp'), may hold values from -6 to 6
- page_table: int32 [128, 6], P('req'), may hold values from 0 to 5, each once within a row
- assignment: int32 [128], P('req'), may hold values from 0 to 127, each once
- lengths: int32 [128], replicated, may hold values from 1 to 768, 24576 in all
- lambda_vectors: float32 [4, 128], replicated, may hold values from -0.4 to 0.4
- subln_gain: float32 [256], replicated, may hold values from 0.5 to 1.5
- residual: bfloat16 [32768, 2048], P('req', 'mlp'), may hold values from -70 to 70
- out_weight: bfloat16 [2048, 2048], P('req', 'mlp'), may hold values from -0.125 to 0.125
- norm_gain: float32 [2048], replicated, may hold values from 0.5 to 1.5
- gate_weight: bfloat16 [2048, 3072], P('req', 'mlp'), may hold values from -0.125 to 0.125
- up_weight: bfloat16 [2048, 3072], P('req', 'mlp'), may hold values from -0.125 to 0.125
- down_weight_t: bfloat16 [2048, 3072], P('req', 'mlp'), may hold values from -0.109375 to 0.109375
Outputs:
- layer_out: bfloat16 [32768, 2048], P('req', 'mlp')
The draws below stay inside these ranges and needn't reach their ends.
Inputs may be any that keep to these rules, and one draw needn't show every extreme that they name: `page_table`: row g lists the cache pages of slot g in logical order as offsets from page g * 6; each offset once in a row. `assignment`: every request is served by exactly one slot. `lengths`: indexed by request; some request has exactly 768 cached tokens.
All inputs are finite; a program needn't handle non-finite values.
Results may differ from the reference program's by a relative error of at most 0.011.
Values may be sent and summed in bfloat16 or wider, within the bound.
No kernel may reach another device: no remote copies, remote signals or barrier semaphores. Data moves between devices by JAX's collectives and lax.ppermute only.
A program may use at most 64 MiB of HBM per device.

```python
import math
import jax
import jax.numpy as jnp
import numpy as np
from jax import lax

D = 2048
HEADS = 8
HALF = 128
FFW = 3072
PAGE = 128
MAXP = 6
NEW = 256
REQS = 128
TOKENS = 32768
POOL = 768
N_MLP = 4


def draw_queries(key, part):
    values = jnp.clip(jax.random.normal(jax.random.fold_in(key, 11), (TOKENS, HEADS, 2 * HALF), jnp.float32), -6.0, 6.0)
    return values.astype(jnp.bfloat16)


def draw_new_kv(key, part):
    values = jnp.clip(jax.random.normal(jax.random.fold_in(key, 12), (TOKENS, HEADS, 4 * HALF), jnp.float32), -6.0, 6.0)
    return values.astype(jnp.bfloat16)


def draw_residual(key, part):
    row_key = jax.random.fold_in(key, 21)
    col_key = jax.random.fold_in(key, 22)
    val_key = jax.random.fold_in(key, 23)
    columns = jnp.arange(D, dtype=jnp.float32) / D
    col_scale = 0.3 * 10.0 ** (columns + 0.2 * jax.random.uniform(col_key, (D,), jnp.float32) - 0.1)
    row_scale = 10.0 ** (jax.random.uniform(row_key, (TOKENS, 1), jnp.float32) - 0.5)
    values = jnp.clip(jax.random.normal(val_key, (TOKENS, D), jnp.float32), -6.0, 6.0)
    return (values * col_scale * row_scale).astype(jnp.bfloat16)


def block_scale(stream_key, dims, shards, least, largest):
    def one(axis_at, blocks):
        draws = jax.random.uniform(jax.random.fold_in(jax.random.fold_in(stream_key, 6), axis_at), (blocks,), jnp.float32, least / len(shards), largest / len(shards))
        return jnp.repeat(jnp.exp(draws), dims[axis_at] // blocks).reshape((-1,) + (1,) * (len(dims) - axis_at - 1))

    gain = one(*shards[0])
    for cut in shards[1:]:
        gain = gain * one(*cut)
    return gain


def split_up(amount, total, reach, lean):
    loads = [(1 << 20) // math.isqrt(standing ** lean) + 1 for standing in range(2, amount + 1)]
    spare, holding = total - reach - (amount - 1), [1] * (amount - 1)
    while spare > 0:
        candidates = [i for i in range(amount - 1) if holding[i] < reach]
        mass, remaining = sum([loads[i] for i in candidates]), spare
        for i in candidates:
            addition = min(reach - holding[i], max(1, remaining * loads[i] // mass), spare)
            holding[i] = holding[i] + addition
            spare = spare - addition
    return np.array([reach] + holding)


def ragged(own_key, number_of, total, reach, slope):
    if number_of == 2:
        one = jax.random.randint(own_key, (), max(1, total - reach), min(reach, total - 1) + 1)
        return jnp.stack([one, total - one])
    sizes = jnp.asarray(split_up(number_of, total, reach, slope), jnp.int32)
    couples = (number_of - 1) // 2
    donor, sink = sizes[1:1 + 2 * couples:2], sizes[2:2 + 2 * couples:2]
    margin = jnp.minimum(donor - 1, reach - sink)
    passed = jax.random.randint(jax.random.fold_in(own_key, 1), (couples,), 0, 1 << 20) % (margin + 1)
    sizes = sizes.at[1:1 + 2 * couples:2].set(donor - passed).at[2:2 + 2 * couples:2].set(sink + passed)
    return sizes[jax.random.permutation(jax.random.fold_in(own_key, 2), number_of)]


def scatter_about(stream_key, shape, width, limit, split=(), kind=jnp.bfloat16):
    factor_of = block_scale(stream_key, shape, split, -0.22, 0.18) if split else 1.0
    entries = jax.random.normal(stream_key, shape, jnp.float32) * width * factor_of
    return jnp.minimum(jnp.maximum(entries, -limit), limit).astype(kind)


def setup_inputs(seed: int = 0) -> dict:
    key_of = jax.random.split(jax.random.key(seed), 15)
    return {
        "queries": draw_queries(jax.random.fold_in(key_of[14], 71), 0),
        "new_kv": draw_new_kv(jax.random.fold_in(key_of[14], 71), 0),
        "cache_pool": scatter_about(key_of[2], (POOL, PAGE, HEADS, 4 * HALF), 1.0, 6.0, ((0, 128), (2, 4))),
        "page_table": jax.vmap(lambda own: jax.random.permutation(own, MAXP))(jax.random.split(key_of[3], REQS)).reshape((REQS, MAXP)).astype(jnp.int32),
        "assignment": jax.random.permutation(key_of[4], REQS).astype(jnp.int32),
        "lengths": ragged(key_of[5], REQS, REQS * MAXP * PAGE // 4, MAXP * PAGE, 2).astype(jnp.int32),
        "lambda_vectors": scatter_about(key_of[6], (4, HALF), 0.1, 0.4, (), jnp.float32),
        "subln_gain": jnp.clip(1.0 + 0.1 * jax.random.normal(key_of[7], (2 * HALF,), jnp.float32), 0.5, 1.5),
        "residual": draw_residual(jax.random.fold_in(key_of[14], 71), 0),
        "out_weight": scatter_about(key_of[9], (2 * HEADS * HALF, D), (2 * HEADS * HALF) ** -0.5, 0.125, ((0, 128), (1, 4))),
        "norm_gain": jnp.clip(1.0 + 0.1 * jax.random.normal(key_of[10], (D,), jnp.float32), 0.5, 1.5),
        "gate_weight": scatter_about(key_of[11], (D, FFW), D ** -0.5, 0.125, ((0, 128), (1, 4))),
        "up_weight": scatter_about(key_of[12], (D, FFW), D ** -0.5, 0.125, ((0, 128), (1, 4))),
        "down_weight_t": scatter_about(key_of[13], (D, FFW), FFW ** -0.5, 0.109375, ((0, 128), (1, 4))),
    }


NEG_FILL = -1e+30
LAMBDA_BASE = 0.2

def one_map(query_rows, key_half, value_rows, visible):
    score = jnp.einsum('nhd,khd->nhk', query_rows.astype(jnp.float32), key_half.astype(jnp.float32)) * HALF ** (-0.5)
    score = jnp.where(visible[:, None, :], score, NEG_FILL)
    row_max = lax.optimization_barrier(jnp.max(score, axis=2, keepdims=True))
    exp_terms = jnp.where(visible[:, None, :], jnp.exp(score - row_max), 0.0)
    exp_total = lax.optimization_barrier(jnp.sum(exp_terms, axis=2))
    rounded = lax.optimization_barrier(exp_terms.astype(jnp.bfloat16))
    mixed_vals = jnp.einsum('nhk,khd->nhd', rounded.astype(jnp.float32), value_rows.astype(jnp.float32))
    return mixed_vals / exp_total[:, :, None]

def reference(queries, new_kv, cache_pool, page_table, assignment, lengths, lambda_vectors, subln_gain, residual, out_weight, norm_gain, gate_weight, up_weight, down_weight_t):
    lambda_now = jnp.exp(jnp.sum(lambda_vectors[0] * lambda_vectors[1])) - jnp.exp(jnp.sum(lambda_vectors[2] * lambda_vectors[3])) + LAMBDA_BASE
    cache_len = MAXP * PAGE
    group_size = FFW // N_MLP

    def one_slot(slot_index):
        row_start = slot_index * NEW
        q_rows = lax.dynamic_slice_in_dim(queries, row_start, NEW, 0)
        kv_rows = lax.dynamic_slice_in_dim(new_kv, row_start, NEW, 0)
        slot_pages = lax.dynamic_slice_in_dim(cache_pool, slot_index * MAXP, MAXP, 0)
        table_row = lax.dynamic_index_in_dim(page_table, slot_index, 0, keepdims=False)
        cached = lengths[assignment[slot_index]]
        cached_rows = slot_pages[table_row].reshape(cache_len, HEADS, 4 * HALF)
        key_rows = jnp.concatenate([cached_rows, kv_rows], axis=0)
        positions = jnp.arange(cache_len, dtype=jnp.int32)
        token_pos = jnp.arange(NEW, dtype=jnp.int32)
        visible = jnp.concatenate([jnp.broadcast_to((positions < cached)[None, :], (NEW, cache_len)), token_pos[None, :] <= token_pos[:, None]], axis=1)
        value_rows = key_rows[:, :, 2 * HALF:]
        map_one = one_map(q_rows[:, :, :HALF], key_rows[:, :, :HALF], value_rows, visible)
        map_two = one_map(q_rows[:, :, HALF:], key_rows[:, :, HALF:2 * HALF], value_rows, visible)
        mix_out = map_one - lambda_now * map_two
        mix_out = mix_out * lax.rsqrt(lax.optimization_barrier(jnp.mean(mix_out * mix_out, axis=2, keepdims=True)) + 1e-05) * subln_gain * (1.0 - LAMBDA_BASE)
        attn_out = mix_out.astype(jnp.bfloat16).reshape(NEW, HEADS * 2 * HALF)
        x_rows = lax.dynamic_slice_in_dim(residual, row_start, NEW, 0)
        stream = (x_rows.astype(jnp.float32) + jnp.dot(attn_out, out_weight, preferred_element_type=jnp.float32)).astype(jnp.bfloat16)
        stream_f = lax.optimization_barrier(stream).astype(jnp.float32)
        normed = (stream_f * lax.rsqrt(lax.optimization_barrier(jnp.mean(stream_f * stream_f, axis=1, keepdims=True)) + 1e-05) * norm_gain).astype(jnp.bfloat16)
        gate_value = jnp.dot(normed, gate_weight, preferred_element_type=jnp.float32)
        up_value = jnp.dot(normed, up_weight, preferred_element_type=jnp.float32)
        hidden_act = (jax.nn.silu(gate_value) * up_value).astype(jnp.bfloat16)
        down_sum = jnp.zeros((NEW, D), jnp.float32)
        for group_index in range(N_MLP):
            group_lo = group_index * group_size
            group_hi = group_lo + group_size
            group_part = lax.dot_general(hidden_act[:, group_lo:group_hi], down_weight_t[:, group_lo:group_hi], (((1,), (1,)), ((), ())), preferred_element_type=jnp.float32)
            down_sum = down_sum + lax.optimization_barrier(group_part.astype(jnp.bfloat16)).astype(jnp.float32)
        return (stream_f + down_sum).astype(jnp.bfloat16)
    outputs = lax.map(one_slot, jnp.arange(REQS, dtype=jnp.int32))
    return outputs.reshape(TOKENS, D)
```

```python
import jax
import jax.numpy as jnp
from jax import lax
from jax.sharding import PartitionSpec as P

D = 2048


NEG_FILL = -1e30
LAMBDA_BASE = 0.2


def map_block(carried, query_rows, key_half, value_rows, visible, score_scale):
    running_max, running_sum, running_acc = carried
    score = (
        jnp.einsum("nhd,khd->nhk", query_rows, key_half, preferred_element_type=jnp.float32)
        * score_scale
    )
    score = jnp.where(visible[:, None, :], score, NEG_FILL)
    newest = jnp.maximum(running_max, jnp.max(score, axis=2))
    exp_terms = jnp.where(visible[:, None, :], jnp.exp(score - newest[:, :, None]), 0.0)
    shrink = jnp.exp(running_max - newest)
    running_sum = running_sum * shrink + jnp.sum(exp_terms, axis=2)
    running_acc = running_acc * shrink[:, :, None] + jnp.einsum(
        "nhk,khd->nhd",
        exp_terms.astype(jnp.bfloat16),
        value_rows,
        preferred_element_type=jnp.float32,
    )
    return (newest, running_sum, running_acc)


def both_maps(carried, query_rows, key_rows, visible, half_size):
    score_scale = half_size ** (-0.5)
    value_rows = key_rows[:, :, 2 * half_size :]
    map_one = map_block(
        carried[0],
        query_rows[:, :, :half_size],
        key_rows[:, :, :half_size],
        value_rows,
        visible,
        score_scale,
    )
    map_two = map_block(
        carried[1],
        query_rows[:, :, half_size:],
        key_rows[:, :, half_size : 2 * half_size],
        value_rows,
        visible,
        score_scale,
    )
    return (map_one, map_two)


def attend(
    queries, new_kv, cache_pool, page_table, assignment, lengths, lambda_vectors, subln_gain
):
    row_count, head_count, value_width = queries.shape
    half_size = value_width // 2
    page_len = cache_pool.shape[1]
    request = assignment[0]
    cached = jnp.sum(
        jnp.where(jnp.arange(lengths.shape[0], dtype=jnp.int32) == request, lengths, 0)
    )

    def fresh_state():
        return (
            jnp.full((row_count, head_count), NEG_FILL, jnp.float32),
            jnp.zeros((row_count, head_count), jnp.float32),
            jnp.zeros((row_count, head_count, value_width), jnp.float32),
        )

    table_row = page_table[0]

    def page_step(page_index, carried):
        physical = table_row[page_index]
        page_rows = lax.dynamic_index_in_dim(cache_pool, physical, 0, keepdims=False)
        positions = page_index * page_len + jnp.arange(page_len, dtype=jnp.int32)
        visible = jnp.broadcast_to((positions < cached)[None, :], (row_count, page_len))
        return both_maps(carried, queries, page_rows, visible, half_size)

    page_count = (cached + page_len - 1) // page_len
    carried = lax.fori_loop(jnp.int32(0), page_count, page_step, (fresh_state(), fresh_state()))
    token_pos = jnp.arange(row_count, dtype=jnp.int32)
    carried = both_maps(
        carried, queries, new_kv, token_pos[None, :] <= token_pos[:, None], half_size
    )
    lambda_now = (
        jnp.exp(jnp.sum(lambda_vectors[0] * lambda_vectors[1]))
        - jnp.exp(jnp.sum(lambda_vectors[2] * lambda_vectors[3]))
        + LAMBDA_BASE
    )
    mix_out = (
        carried[0][2] / carried[0][1][:, :, None]
        - lambda_now * carried[1][2] / carried[1][1][:, :, None]
    )
    mix_out = (
        mix_out
        * lax.rsqrt(jnp.mean(mix_out * mix_out, axis=2, keepdims=True) + 1e-05)
        * subln_gain
        * (1.0 - LAMBDA_BASE)
    )
    return mix_out.astype(jnp.bfloat16).reshape(row_count, head_count * value_width)


def per_device(
    queries,
    new_kv,
    cache_pool,
    page_table,
    assignment,
    lengths,
    lambda_vectors,
    subln_gain,
    residual,
    out_weight,
    norm_gain,
    gate_weight,
    up_weight,
    down_weight_t,
):
    widths = [out_weight.shape[1], gate_weight.shape[1], up_weight.shape[1], down_weight_t.shape[1]]
    packed = jnp.concatenate([out_weight, gate_weight, up_weight, down_weight_t], axis=1)
    gathered = lax.all_gather(packed, "req", axis=0, tiled=True)
    bounds = [0]
    for w in widths:
        bounds.append(bounds[-1] + w)
    out_full, gate_full, up_full, down_full = [
        gathered[:, bounds[i] : bounds[i + 1]] for i in range(4)
    ]
    attn_out = attend(
        queries, new_kv, cache_pool, page_table, assignment, lengths, lambda_vectors, subln_gain
    )
    heads_all = lax.all_gather(attn_out, "mlp", axis=1, tiled=True)
    projected = jnp.dot(heads_all, out_full, preferred_element_type=jnp.float32)
    stream = (residual.astype(jnp.float32) + projected).astype(jnp.bfloat16)
    stream_all = lax.all_gather(stream, "mlp", axis=1, tiled=True).astype(jnp.float32)
    squares = jnp.sum(stream_all * stream_all, axis=1, keepdims=True)
    normed = (stream_all * lax.rsqrt(squares / D + 1e-05) * norm_gain).astype(jnp.bfloat16)
    gate_value = jnp.dot(normed, gate_full, preferred_element_type=jnp.float32)
    up_value = jnp.dot(normed, up_full, preferred_element_type=jnp.float32)
    hidden_act = (jax.nn.silu(gate_value) * up_value).astype(jnp.bfloat16)
    partial_value = lax.dot_general(
        hidden_act,
        down_full,
        (((1,), (1,)), ((), ())),
        preferred_element_type=jnp.float32,
    )
    summed = lax.psum_scatter(
        partial_value.astype(jnp.bfloat16), "mlp", scatter_dimension=1, tiled=True
    ).astype(jnp.float32)
    return (stream.astype(jnp.float32) + summed).astype(jnp.bfloat16)


def solution(mesh):
    in_specs = (
        P("req", "mlp", None),
        P("req", "mlp", None),
        P("req", None, "mlp", None),
        P("req", None),
        P("req"),
        P(),
        P(),
        P(),
        P("req", "mlp"),
        P("req", "mlp"),
        P(),
        P("req", "mlp"),
        P("req", "mlp"),
        P("req", "mlp"),
    )
    out_specs = P("req", "mlp")
    return jax.shard_map(
        per_device, mesh=mesh, in_specs=in_specs, out_specs=out_specs, check_vma=False
    )
```

```python
import jax
import jax.numpy as jnp
from jax import lax
from jax.sharding import PartitionSpec as P

D = 2048


NEG_FILL = -1e30
LAMBDA_BASE = 0.2


def map_block(carried, query_rows, key_half, value_rows, visible, score_scale):
    running_max, running_sum, running_acc = carried
    score = (
        jnp.einsum("nhd,khd->nhk", query_rows, key_half, preferred_element_type=jnp.float32)
        * score_scale
    )
    score = jnp.where(visible[:, None, :], score, NEG_FILL)
    newest = jnp.maximum(running_max, jnp.max(score, axis=2))
    exp_terms = jnp.where(visible[:, None, :], jnp.exp(score - newest[:, :, None]), 0.0)
    shrink = jnp.exp(running_max - newest)
    running_sum = running_sum * shrink + jnp.sum(exp_terms, axis=2)
    running_acc = running_acc * shrink[:, :, None] + jnp.einsum(
        "nhk,khd->nhd",
        exp_terms.astype(jnp.bfloat16),
        value_rows,
        preferred_element_type=jnp.float32,
    )
    return (newest, running_sum, running_acc)


def both_maps(carried, query_rows, key_rows, visible, half_size):
    score_scale = half_size ** (-0.5)
    value_rows = key_rows[:, :, 2 * half_size :]
    map_one = map_block(
        carried[0],
        query_rows[:, :, :half_size],
        key_rows[:, :, :half_size],
        value_rows,
        visible,
        score_scale,
    )
    map_two = map_block(
        carried[1],
        query_rows[:, :, half_size:],
        key_rows[:, :, half_size : 2 * half_size],
        value_rows,
        visible,
        score_scale,
    )
    return (map_one, map_two)


def attend(
    queries, new_kv, cache_pool, page_table, assignment, lengths, lambda_vectors, subln_gain
):
    row_count, head_count, value_width = queries.shape
    half_size = value_width // 2
    page_len = cache_pool.shape[1]
    request = assignment[0]
    cached = jnp.sum(
        jnp.where(jnp.arange(lengths.shape[0], dtype=jnp.int32) == request, lengths, 0)
    )

    def fresh_state():
        return (
            jnp.full((row_count, head_count), NEG_FILL, jnp.float32),
            jnp.zeros((row_count, head_count), jnp.float32),
            jnp.zeros((row_count, head_count, value_width), jnp.float32),
        )

    table_row = page_table[0]

    def page_step(page_index, carried):
        physical = table_row[page_index]
        page_rows = lax.dynamic_index_in_dim(cache_pool, physical, 0, keepdims=False)
        positions = page_index * page_len + jnp.arange(page_len, dtype=jnp.int32)
        visible = jnp.broadcast_to((positions < cached)[None, :], (row_count, page_len))
        return both_maps(carried, queries, page_rows, visible, half_size)

    page_count = (cached + page_len - 1) // page_len
    carried = lax.fori_loop(jnp.int32(0), page_count, page_step, (fresh_state(), fresh_state()))
    token_pos = jnp.arange(row_count, dtype=jnp.int32)
    carried = both_maps(
        carried, queries, new_kv, token_pos[None, :] <= token_pos[:, None], half_size
    )
    lambda_now = (
        jnp.exp(jnp.sum(lambda_vectors[0] * lambda_vectors[1]))
        - jnp.exp(jnp.sum(lambda_vectors[2] * lambda_vectors[3]))
        + LAMBDA_BASE
    )
    mix_out = (
        carried[0][2] / carried[0][1][:, :, None]
        - lambda_now * carried[1][2] / carried[1][1][:, :, None]
    )
    mix_out = (
        mix_out
        * lax.rsqrt(jnp.mean(mix_out * mix_out, axis=2, keepdims=True) + 1e-05)
        * subln_gain
        * (1.0 - LAMBDA_BASE)
    )
    return mix_out.astype(jnp.bfloat16).reshape(row_count, head_count * value_width)


def mlp_gather(block, axis_size):
    index = lax.axis_index("mlp")
    pieces = [block]
    for shift in range(1, axis_size):
        pieces.append(
            lax.ppermute(block, "mlp", [(i, (i + shift) % axis_size) for i in range(axis_size)])
        )
    stacked = jnp.stack(pieces, axis=0)
    source_of = (index - jnp.arange(axis_size, dtype=jnp.int32)) % axis_size
    gathered = jnp.take(stacked, source_of, axis=0)
    return jnp.concatenate([gathered[k] for k in range(axis_size)], axis=1)


def mlp_reduce_scatter(partial_value, axis_size):
    index = lax.axis_index("mlp")
    width = partial_value.shape[1] // axis_size
    blocks = partial_value.reshape(partial_value.shape[0], axis_size, width)
    total = lax.dynamic_index_in_dim(blocks, index, 1, keepdims=False).astype(jnp.float32)
    for shift in range(1, axis_size):
        target = (index + shift) % axis_size
        outgoing = lax.dynamic_index_in_dim(blocks, target, 1, keepdims=False)
        incoming = lax.ppermute(
            outgoing, "mlp", [(i, (i + shift) % axis_size) for i in range(axis_size)]
        )
        total = total + incoming.astype(jnp.float32)
    return total


def per_device(
    queries,
    new_kv,
    cache_pool,
    page_table,
    assignment,
    lengths,
    lambda_vectors,
    subln_gain,
    residual,
    out_weight,
    norm_gain,
    gate_weight,
    up_weight,
    down_weight_t,
):
    widths = [out_weight.shape[1], gate_weight.shape[1], up_weight.shape[1], down_weight_t.shape[1]]
    packed = jnp.concatenate([out_weight, gate_weight, up_weight, down_weight_t], axis=1)
    gathered = lax.all_gather(packed, "req", axis=0, tiled=True)
    bounds = [0]
    for w in widths:
        bounds.append(bounds[-1] + w)
    out_full, gate_full, up_full, down_full = [
        gathered[:, bounds[i] : bounds[i + 1]] for i in range(4)
    ]
    attn_out = attend(
        queries, new_kv, cache_pool, page_table, assignment, lengths, lambda_vectors, subln_gain
    )
    mlp_size = D // residual.shape[1]
    heads_all = mlp_gather(attn_out, mlp_size)
    projected = jnp.dot(heads_all, out_full, preferred_element_type=jnp.float32)
    stream = (residual.astype(jnp.float32) + projected).astype(jnp.bfloat16)
    stream_all = mlp_gather(stream, mlp_size).astype(jnp.float32)
    squares = jnp.sum(stream_all * stream_all, axis=1, keepdims=True)
    normed = (stream_all * lax.rsqrt(squares / D + 1e-05) * norm_gain).astype(jnp.bfloat16)
    gate_value = jnp.dot(normed, gate_full, preferred_element_type=jnp.float32)
    up_value = jnp.dot(normed, up_full, preferred_element_type=jnp.float32)
    hidden_act = (jax.nn.silu(gate_value) * up_value).astype(jnp.bfloat16)
    partial_value = lax.dot_general(
        hidden_act,
        down_full,
        (((1,), (1,)), ((), ())),
        preferred_element_type=jnp.float32,
    )
    summed = mlp_reduce_scatter(partial_value.astype(jnp.bfloat16), mlp_size)
    return (stream.astype(jnp.float32) + summed).astype(jnp.bfloat16)


def solution(mesh):
    in_specs = (
        P("req", "mlp", None),
        P("req", "mlp", None),
        P("req", None, "mlp", None),
        P("req", None),
        P("req"),
        P(),
        P(),
        P(),
        P("req", "mlp"),
        P("req", "mlp"),
        P(),
        P("req", "mlp"),
        P("req", "mlp"),
        P("req", "mlp"),
    )
    out_specs = P("req", "mlp")
    return jax.shard_map(
        per_device, mesh=mesh, in_specs=in_specs, out_specs=out_specs, check_vma=False
    )
```

```python
import jax
import jax.numpy as jnp
from jax import lax
from jax.sharding import PartitionSpec as P

D = 2048


NEG_FILL = -1e30
LAMBDA_BASE = 0.2


def map_block(carried, query_rows, key_half, value_rows, visible, score_scale):
    running_max, running_sum, running_acc = carried
    score = (
        jnp.einsum("nhd,khd->nhk", query_rows, key_half, preferred_element_type=jnp.float32)
        * score_scale
    )
    score = jnp.where(visible[:, None, :], score, NEG_FILL)
    newest = jnp.maximum(running_max, jnp.max(score, axis=2))
    exp_terms = jnp.where(visible[:, None, :], jnp.exp(score - newest[:, :, None]), 0.0)
    shrink = jnp.exp(running_max - newest)
    running_sum = running_sum * shrink + jnp.sum(exp_terms, axis=2)
    running_acc = running_acc * shrink[:, :, None] + jnp.einsum(
        "nhk,khd->nhd",
        exp_terms.astype(jnp.bfloat16),
        value_rows,
        preferred_element_type=jnp.float32,
    )
    return (newest, running_sum, running_acc)


def both_maps(carried, query_rows, key_rows, visible, half_size):
    score_scale = half_size ** (-0.5)
    value_rows = key_rows[:, :, 2 * half_size :]
    map_one = map_block(
        carried[0],
        query_rows[:, :, :half_size],
        key_rows[:, :, :half_size],
        value_rows,
        visible,
        score_scale,
    )
    map_two = map_block(
        carried[1],
        query_rows[:, :, half_size:],
        key_rows[:, :, half_size : 2 * half_size],
        value_rows,
        visible,
        score_scale,
    )
    return (map_one, map_two)


def attend(
    queries, new_kv, cache_pool, page_table, assignment, lengths, lambda_vectors, subln_gain
):
    row_count, head_count, value_width = queries.shape
    half_size = value_width // 2
    page_len = cache_pool.shape[1]
    request = assignment[0]
    cached = jnp.sum(
        jnp.where(jnp.arange(lengths.shape[0], dtype=jnp.int32) == request, lengths, 0)
    )

    def fresh_state():
        return (
            jnp.full((row_count, head_count), NEG_FILL, jnp.float32),
            jnp.zeros((row_count, head_count), jnp.float32),
            jnp.zeros((row_count, head_count, value_width), jnp.float32),
        )

    table_row = page_table[0]

    def page_step(page_index, carried):
        physical = table_row[page_index]
        page_rows = lax.dynamic_index_in_dim(cache_pool, physical, 0, keepdims=False)
        positions = page_index * page_len + jnp.arange(page_len, dtype=jnp.int32)
        visible = jnp.broadcast_to((positions < cached)[None, :], (row_count, page_len))
        return both_maps(carried, queries, page_rows, visible, half_size)

    page_count = (cached + page_len - 1) // page_len
    carried = lax.fori_loop(jnp.int32(0), page_count, page_step, (fresh_state(), fresh_state()))
    token_pos = jnp.arange(row_count, dtype=jnp.int32)
    carried = both_maps(
        carried, queries, new_kv, token_pos[None, :] <= token_pos[:, None], half_size
    )
    lambda_now = (
        jnp.exp(jnp.sum(lambda_vectors[0] * lambda_vectors[1]))
        - jnp.exp(jnp.sum(lambda_vectors[2] * lambda_vectors[3]))
        + LAMBDA_BASE
    )
    mix_out = (
        carried[0][2] / carried[0][1][:, :, None]
        - lambda_now * carried[1][2] / carried[1][1][:, :, None]
    )
    mix_out = (
        mix_out
        * lax.rsqrt(jnp.mean(mix_out * mix_out, axis=2, keepdims=True) + 1e-05)
        * subln_gain
        * (1.0 - LAMBDA_BASE)
    )
    return mix_out.astype(jnp.bfloat16).reshape(row_count, head_count * value_width)


def mlp_gather(block, axis_size):
    index = lax.axis_index("mlp")
    pieces = [block]
    for shift in range(1, axis_size):
        pieces.append(
            lax.ppermute(block, "mlp", [(i, (i + shift) % axis_size) for i in range(axis_size)])
        )
    stacked = jnp.stack(pieces, axis=0)
    source_of = (index - jnp.arange(axis_size, dtype=jnp.int32)) % axis_size
    gathered = jnp.take(stacked, source_of, axis=0)
    return jnp.concatenate([gathered[k] for k in range(axis_size)], axis=1)


def mlp_reduce_scatter(partial_value, axis_size):
    index = lax.axis_index("mlp")
    width = partial_value.shape[1] // axis_size
    blocks = partial_value.reshape(partial_value.shape[0], axis_size, width)
    total = lax.dynamic_index_in_dim(blocks, index, 1, keepdims=False).astype(jnp.float32)
    for shift in range(1, axis_size):
        target = (index + shift) % axis_size
        outgoing = lax.dynamic_index_in_dim(blocks, target, 1, keepdims=False)
        incoming = lax.ppermute(
            outgoing, "mlp", [(i, (i + shift) % axis_size) for i in range(axis_size)]
        )
        total = total + incoming.astype(jnp.float32)
    return total


DOUBLING_BITS = (4, 3, 6, 2, 5, 1, 0)


def req_gather_by_permutes(block):
    size = lax.axis_size("req")
    index = lax.axis_index("req")
    rows, width = block.shape
    bits = [b for b in DOUBLING_BITS if (1 << b) < size]
    out = block
    for bit in bits:
        partner = lax.ppermute(out, "req", [(r, r ^ (1 << bit)) for r in range(size)])
        upper = (index >> bit) & 1
        out = jnp.where(
            upper == 1,
            jnp.concatenate([partner, out], axis=0),
            jnp.concatenate([out, partner], axis=0),
        )
    count = len(bits)
    out = out.reshape((2,) * count + (rows, width))
    axis_of_bit = {bits[count - 1 - j]: j for j in range(count)}
    order = [axis_of_bit[b] for b in range(count - 1, -1, -1)]
    out = out.transpose(order + [count, count + 1])
    return out.reshape(size * rows, width)


def per_device(
    queries,
    new_kv,
    cache_pool,
    page_table,
    assignment,
    lengths,
    lambda_vectors,
    subln_gain,
    residual,
    out_weight,
    norm_gain,
    gate_weight,
    up_weight,
    down_weight_t,
):
    widths = [gate_weight.shape[1], up_weight.shape[1], down_weight_t.shape[1]]
    packed = jnp.concatenate([gate_weight, up_weight, down_weight_t], axis=1)
    gathered = lax.all_gather(packed, "req", axis=0, tiled=True)
    bounds = [0]
    for w in widths:
        bounds.append(bounds[-1] + w)
    gate_full, up_full, down_full = [
        gathered[:, bounds[i] : bounds[i + 1]] for i in range(3)
    ]
    out_full = req_gather_by_permutes(out_weight)
    attn_out = attend(
        queries, new_kv, cache_pool, page_table, assignment, lengths, lambda_vectors, subln_gain
    )
    mlp_size = D // residual.shape[1]
    heads_all = mlp_gather(attn_out, mlp_size)
    projected = jnp.dot(heads_all, out_full, preferred_element_type=jnp.float32)
    stream = (residual.astype(jnp.float32) + projected).astype(jnp.bfloat16)
    stream_all = mlp_gather(stream, mlp_size).astype(jnp.float32)
    squares = jnp.sum(stream_all * stream_all, axis=1, keepdims=True)
    normed = (stream_all * lax.rsqrt(squares / D + 1e-05) * norm_gain).astype(jnp.bfloat16)
    gate_value = jnp.dot(normed, gate_full, preferred_element_type=jnp.float32)
    up_value = jnp.dot(normed, up_full, preferred_element_type=jnp.float32)
    hidden_act = (jax.nn.silu(gate_value) * up_value).astype(jnp.bfloat16)
    partial_value = lax.dot_general(
        hidden_act,
        down_full,
        (((1,), (1,)), ((), ())),
        preferred_element_type=jnp.float32,
    )
    summed = mlp_reduce_scatter(partial_value.astype(jnp.bfloat16), mlp_size)
    return (stream.astype(jnp.float32) + summed).astype(jnp.bfloat16)


def solution(mesh):
    in_specs = (
        P("req", "mlp", None),
        P("req", "mlp", None),
        P("req", None, "mlp", None),
        P("req", None),
        P("req"),
        P(),
        P(),
        P(),
        P("req", "mlp"),
        P("req", "mlp"),
        P(),
        P("req", "mlp"),
        P("req", "mlp"),
        P("req", "mlp"),
    )
    out_specs = P("req", "mlp")
    return jax.shard_map(
        per_device, mesh=mesh, in_specs=in_specs, out_specs=out_specs, check_vma=False
    )
```

```python
import jax
import jax.numpy as jnp
from jax import lax
from jax.sharding import PartitionSpec as P

D = 2048


NEG_FILL = -1e30
LAMBDA_BASE = 0.2


def attend(
    queries, new_kv, cache_pool, page_table, assignment, lengths, lambda_vectors, subln_gain
):
    row_count, head_count, value_width = queries.shape
    half_size = value_width // 2
    score_scale = half_size ** (-0.5)
    request = assignment[0]
    cached = jnp.sum(
        jnp.where(jnp.arange(lengths.shape[0], dtype=jnp.int32) == request, lengths, 0)
    )
    pages = jnp.take(cache_pool, page_table[0], axis=0)
    cached_rows = pages.reshape(-1, head_count, cache_pool.shape[3])
    cache_len = cached_rows.shape[0]
    key_rows = jnp.concatenate([cached_rows, new_kv], axis=0)
    positions = jnp.arange(cache_len, dtype=jnp.int32)
    token_pos = jnp.arange(row_count, dtype=jnp.int32)
    visible = jnp.concatenate(
        [
            jnp.broadcast_to((positions < cached)[None, :], (row_count, cache_len)),
            token_pos[None, :] <= token_pos[:, None],
        ],
        axis=1,
    )
    value_rows = key_rows[:, :, 2 * half_size :]

    def one_map(query_rows, key_half):
        score = (
            jnp.einsum("nhd,khd->nhk", query_rows, key_half, preferred_element_type=jnp.float32)
            * score_scale
        )
        score = jnp.where(visible[:, None, :], score, NEG_FILL)
        row_max = jnp.max(score, axis=2, keepdims=True)
        exp_terms = jnp.where(visible[:, None, :], jnp.exp(score - row_max), 0.0)
        exp_total = jnp.sum(exp_terms, axis=2)
        mixed = jnp.einsum(
            "nhk,khd->nhd",
            exp_terms.astype(jnp.bfloat16),
            value_rows,
            preferred_element_type=jnp.float32,
        )
        return mixed / exp_total[:, :, None]

    map_one = one_map(queries[:, :, :half_size], key_rows[:, :, :half_size])
    map_two = one_map(queries[:, :, half_size:], key_rows[:, :, half_size : 2 * half_size])
    lambda_now = (
        jnp.exp(jnp.sum(lambda_vectors[0] * lambda_vectors[1]))
        - jnp.exp(jnp.sum(lambda_vectors[2] * lambda_vectors[3]))
        + LAMBDA_BASE
    )
    mix_out = map_one - lambda_now * map_two
    mix_out = (
        mix_out
        * lax.rsqrt(jnp.mean(mix_out * mix_out, axis=2, keepdims=True) + 1e-05)
        * subln_gain
        * (1.0 - LAMBDA_BASE)
    )
    return mix_out.astype(jnp.bfloat16).reshape(row_count, head_count * value_width)


def mlp_gather(block, axis_size):
    index = lax.axis_index("mlp")
    pieces = [block]
    for shift in range(1, axis_size):
        pieces.append(
            lax.ppermute(block, "mlp", [(i, (i + shift) % axis_size) for i in range(axis_size)])
        )
    stacked = jnp.stack(pieces, axis=0)
    source_of = (index - jnp.arange(axis_size, dtype=jnp.int32)) % axis_size
    gathered = jnp.take(stacked, source_of, axis=0)
    return jnp.concatenate([gathered[k] for k in range(axis_size)], axis=1)


def mlp_reduce_scatter(partial_value, axis_size):
    index = lax.axis_index("mlp")
    width = partial_value.shape[1] // axis_size
    blocks = partial_value.reshape(partial_value.shape[0], axis_size, width)
    total = lax.dynamic_index_in_dim(blocks, index, 1, keepdims=False).astype(jnp.float32)
    for shift in range(1, axis_size):
        target = (index + shift) % axis_size
        outgoing = lax.dynamic_index_in_dim(blocks, target, 1, keepdims=False)
        incoming = lax.ppermute(
            outgoing, "mlp", [(i, (i + shift) % axis_size) for i in range(axis_size)]
        )
        total = total + incoming.astype(jnp.float32)
    return total


DOUBLING_BITS = (4, 3, 6, 2, 5, 1, 0)


def req_gather_by_permutes(block):
    size = lax.axis_size("req")
    index = lax.axis_index("req")
    rows, width = block.shape
    bits = [b for b in DOUBLING_BITS if (1 << b) < size]
    out = block
    for bit in bits:
        partner = lax.ppermute(out, "req", [(r, r ^ (1 << bit)) for r in range(size)])
        upper = (index >> bit) & 1
        out = jnp.where(
            upper == 1,
            jnp.concatenate([partner, out], axis=0),
            jnp.concatenate([out, partner], axis=0),
        )
    count = len(bits)
    out = out.reshape((2,) * count + (rows, width))
    axis_of_bit = {bits[count - 1 - j]: j for j in range(count)}
    order = [axis_of_bit[b] for b in range(count - 1, -1, -1)]
    out = out.transpose(order + [count, count + 1])
    return out.reshape(size * rows, width)


def per_device(
    queries,
    new_kv,
    cache_pool,
    page_table,
    assignment,
    lengths,
    lambda_vectors,
    subln_gain,
    residual,
    out_weight,
    norm_gain,
    gate_weight,
    up_weight,
    down_weight_t,
):
    widths = [gate_weight.shape[1], up_weight.shape[1], down_weight_t.shape[1]]
    packed = jnp.concatenate([gate_weight, up_weight, down_weight_t], axis=1)
    gathered = lax.all_gather(packed, "req", axis=0, tiled=True)
    bounds = [0]
    for w in widths:
        bounds.append(bounds[-1] + w)
    gate_full, up_full, down_full = [
        gathered[:, bounds[i] : bounds[i + 1]] for i in range(3)
    ]
    out_full = req_gather_by_permutes(out_weight)
    attn_out = attend(
        queries, new_kv, cache_pool, page_table, assignment, lengths, lambda_vectors, subln_gain
    )
    mlp_size = D // residual.shape[1]
    heads_all = mlp_gather(attn_out, mlp_size)
    projected = jnp.dot(heads_all, out_full, preferred_element_type=jnp.float32)
    stream = (residual.astype(jnp.float32) + projected).astype(jnp.bfloat16)
    stream_all = mlp_gather(stream, mlp_size).astype(jnp.float32)
    squares = jnp.sum(stream_all * stream_all, axis=1, keepdims=True)
    normed = (stream_all * lax.rsqrt(squares / D + 1e-05) * norm_gain).astype(jnp.bfloat16)
    gate_value = jnp.dot(normed, gate_full, preferred_element_type=jnp.float32)
    up_value = jnp.dot(normed, up_full, preferred_element_type=jnp.float32)
    hidden_act = (jax.nn.silu(gate_value) * up_value).astype(jnp.bfloat16)
    partial_value = lax.dot_general(
        hidden_act,
        down_full,
        (((1,), (1,)), ((), ())),
        preferred_element_type=jnp.float32,
    )
    summed = mlp_reduce_scatter(partial_value.astype(jnp.bfloat16), mlp_size)
    return (stream.astype(jnp.float32) + summed).astype(jnp.bfloat16)


def solution(mesh):
    in_specs = (
        P("req", "mlp", None),
        P("req", "mlp", None),
        P("req", None, "mlp", None),
        P("req", None),
        P("req"),
        P(),
        P(),
        P(),
        P("req", "mlp"),
        P("req", "mlp"),
        P(),
        P("req", "mlp"),
        P("req", "mlp"),
        P("req", "mlp"),
    )
    out_specs = P("req", "mlp")
    return jax.shard_map(
        per_device, mesh=mesh, in_specs=in_specs, out_specs=out_specs, check_vma=False
    )
```

```python
import jax
import jax.numpy as jnp
from jax import lax
from jax.sharding import PartitionSpec as P

D = 2048


NEG_FILL = -1e30
LAMBDA_BASE = 0.2


def attend(
    queries, new_kv, cache_pool, page_table, assignment, lengths, lambda_vectors, subln_gain
):
    row_count, head_count, value_width = queries.shape
    half_size = value_width // 2
    score_scale = half_size ** (-0.5)
    request = assignment[0]
    cached = jnp.sum(
        jnp.where(jnp.arange(lengths.shape[0], dtype=jnp.int32) == request, lengths, 0)
    )
    pages = jnp.take(cache_pool, page_table[0], axis=0)
    cached_rows = pages.reshape(-1, head_count, cache_pool.shape[3])
    cache_len = cached_rows.shape[0]
    key_rows = jnp.concatenate([cached_rows, new_kv], axis=0)
    positions = jnp.arange(cache_len, dtype=jnp.int32)
    token_pos = jnp.arange(row_count, dtype=jnp.int32)
    visible = jnp.concatenate(
        [
            jnp.broadcast_to((positions < cached)[None, :], (row_count, cache_len)),
            token_pos[None, :] <= token_pos[:, None],
        ],
        axis=1,
    )
    value_rows = key_rows[:, :, 2 * half_size :]

    def one_map(query_rows, key_half):
        score = (
            jnp.einsum("nhd,khd->nhk", query_rows, key_half, preferred_element_type=jnp.float32)
            * score_scale
        )
        score = jnp.where(visible[:, None, :], score, NEG_FILL)
        row_max = jnp.max(score, axis=2, keepdims=True)
        exp_terms = jnp.where(visible[:, None, :], jnp.exp(score - row_max), 0.0)
        exp_total = jnp.sum(exp_terms, axis=2)
        mixed = jnp.einsum(
            "nhk,khd->nhd",
            exp_terms.astype(jnp.bfloat16),
            value_rows,
            preferred_element_type=jnp.float32,
        )
        return mixed / exp_total[:, :, None]

    map_one = one_map(queries[:, :, :half_size], key_rows[:, :, :half_size])
    map_two = one_map(queries[:, :, half_size:], key_rows[:, :, half_size : 2 * half_size])
    lambda_now = (
        jnp.exp(jnp.sum(lambda_vectors[0] * lambda_vectors[1]))
        - jnp.exp(jnp.sum(lambda_vectors[2] * lambda_vectors[3]))
        + LAMBDA_BASE
    )
    mix_out = map_one - lambda_now * map_two
    mix_out = (
        mix_out
        * lax.rsqrt(jnp.mean(mix_out * mix_out, axis=2, keepdims=True) + 1e-05)
        * subln_gain
        * (1.0 - LAMBDA_BASE)
    )
    return mix_out.astype(jnp.bfloat16).reshape(row_count, head_count * value_width)


def mlp_gather(block, axis_size):
    index = lax.axis_index("mlp")
    pieces = [block]
    for shift in range(1, axis_size):
        pieces.append(
            lax.ppermute(block, "mlp", [(i, (i + shift) % axis_size) for i in range(axis_size)])
        )
    stacked = jnp.stack(pieces, axis=0)
    source_of = (index - jnp.arange(axis_size, dtype=jnp.int32)) % axis_size
    gathered = jnp.take(stacked, source_of, axis=0)
    return jnp.concatenate([gathered[k] for k in range(axis_size)], axis=1)


def down_and_scatter(hidden_act, down_full, axis_size):
    index = lax.axis_index("mlp")
    width = down_full.shape[0] // axis_size

    def block_for(target):
        rows = lax.dynamic_slice_in_dim(down_full, target * width, width, 0)
        value = lax.dot_general(
            hidden_act, rows, (((1,), (1,)), ((), ())), preferred_element_type=jnp.float32
        )
        return value.astype(jnp.bfloat16)

    incoming = []
    for shift in range(1, axis_size):
        target = (index + shift) % axis_size
        incoming.append(
            lax.ppermute(
                block_for(target), "mlp", [(i, (i + shift) % axis_size) for i in range(axis_size)]
            )
        )
    total = block_for(index).astype(jnp.float32)
    for received in incoming:
        total = total + received.astype(jnp.float32)
    return total


DOUBLING_BITS = (4, 3, 6, 2, 5, 1, 0)


def req_gather_by_permutes(block):
    size = lax.axis_size("req")
    index = lax.axis_index("req")
    rows, width = block.shape
    bits = [b for b in DOUBLING_BITS if (1 << b) < size]
    out = block
    for bit in bits:
        partner = lax.ppermute(out, "req", [(r, r ^ (1 << bit)) for r in range(size)])
        upper = (index >> bit) & 1
        out = jnp.where(
            upper == 1,
            jnp.concatenate([partner, out], axis=0),
            jnp.concatenate([out, partner], axis=0),
        )
    count = len(bits)
    out = out.reshape((2,) * count + (rows, width))
    axis_of_bit = {bits[count - 1 - j]: j for j in range(count)}
    order = [axis_of_bit[b] for b in range(count - 1, -1, -1)]
    out = out.transpose(order + [count, count + 1])
    return out.reshape(size * rows, width)


def per_device(
    queries,
    new_kv,
    cache_pool,
    page_table,
    assignment,
    lengths,
    lambda_vectors,
    subln_gain,
    residual,
    out_weight,
    norm_gain,
    gate_weight,
    up_weight,
    down_weight_t,
):
    widths = [gate_weight.shape[1], up_weight.shape[1], down_weight_t.shape[1]]
    packed = jnp.concatenate([gate_weight, up_weight, down_weight_t], axis=1)
    gathered = lax.all_gather(packed, "req", axis=0, tiled=True)
    bounds = [0]
    for w in widths:
        bounds.append(bounds[-1] + w)
    gate_full, up_full, down_full = [
        gathered[:, bounds[i] : bounds[i + 1]] for i in range(3)
    ]
    out_full = req_gather_by_permutes(out_weight)
    attn_out = attend(
        queries, new_kv, cache_pool, page_table, assignment, lengths, lambda_vectors, subln_gain
    )
    mlp_size = D // residual.shape[1]
    heads_all = mlp_gather(attn_out, mlp_size)
    projected = jnp.dot(heads_all, out_full, preferred_element_type=jnp.float32)
    stream = (residual.astype(jnp.float32) + projected).astype(jnp.bfloat16)
    stream_all = mlp_gather(stream, mlp_size).astype(jnp.float32)
    squares = jnp.sum(stream_all * stream_all, axis=1, keepdims=True)
    normed = (stream_all * lax.rsqrt(squares / D + 1e-05) * norm_gain).astype(jnp.bfloat16)
    gate_value = jnp.dot(normed, gate_full, preferred_element_type=jnp.float32)
    up_value = jnp.dot(normed, up_full, preferred_element_type=jnp.float32)
    hidden_act = (jax.nn.silu(gate_value) * up_value).astype(jnp.bfloat16)
    summed = down_and_scatter(hidden_act, down_full, mlp_size)
    return (stream.astype(jnp.float32) + summed).astype(jnp.bfloat16)


def solution(mesh):
    in_specs = (
        P("req", "mlp", None),
        P("req", "mlp", None),
        P("req", None, "mlp", None),
        P("req", None),
        P("req"),
        P(),
        P(),
        P(),
        P("req", "mlp"),
        P("req", "mlp"),
        P(),
        P("req", "mlp"),
        P("req", "mlp"),
        P("req", "mlp"),
    )
    out_specs = P("req", "mlp")
    return jax.shard_map(
        per_device, mesh=mesh, in_specs=in_specs, out_specs=out_specs, check_vma=False
    )
```

```python
import jax
import jax.numpy as jnp
from jax import lax
from jax.sharding import Mesh, PartitionSpec as P

D = 2048


NEG_FILL = -1e30
LAMBDA_BASE = 0.2


def attend(
    queries, new_kv, cache_pool, page_table, assignment, lengths, lambda_vectors, subln_gain
):
    row_count, head_count, value_width = queries.shape
    half_size = value_width // 2
    score_scale = half_size ** (-0.5)
    request = assignment[0]
    cached = jnp.sum(
        jnp.where(jnp.arange(lengths.shape[0], dtype=jnp.int32) == request, lengths, 0)
    )
    pages = jnp.take(cache_pool, page_table[0], axis=0)
    cached_rows = pages.reshape(-1, head_count, cache_pool.shape[3])
    cache_len = cached_rows.shape[0]
    key_rows = jnp.concatenate([cached_rows, new_kv], axis=0)
    positions = jnp.arange(cache_len, dtype=jnp.int32)
    token_pos = jnp.arange(row_count, dtype=jnp.int32)
    visible = jnp.concatenate(
        [
            jnp.broadcast_to((positions < cached)[None, :], (row_count, cache_len)),
            token_pos[None, :] <= token_pos[:, None],
        ],
        axis=1,
    )
    value_rows = key_rows[:, :, 2 * half_size :]

    def one_map(query_rows, key_half):
        score = (
            jnp.einsum("nhd,khd->nhk", query_rows, key_half, preferred_element_type=jnp.float32)
            * score_scale
        )
        score = jnp.where(visible[:, None, :], score, NEG_FILL)
        row_max = jnp.max(score, axis=2, keepdims=True)
        exp_terms = jnp.where(visible[:, None, :], jnp.exp(score - row_max), 0.0)
        exp_total = jnp.sum(exp_terms, axis=2)
        mixed = jnp.einsum(
            "nhk,khd->nhd",
            exp_terms.astype(jnp.bfloat16),
            value_rows,
            preferred_element_type=jnp.float32,
        )
        return mixed / exp_total[:, :, None]

    map_one = one_map(queries[:, :, :half_size], key_rows[:, :, :half_size])
    map_two = one_map(queries[:, :, half_size:], key_rows[:, :, half_size : 2 * half_size])
    lambda_now = (
        jnp.exp(jnp.sum(lambda_vectors[0] * lambda_vectors[1]))
        - jnp.exp(jnp.sum(lambda_vectors[2] * lambda_vectors[3]))
        + LAMBDA_BASE
    )
    mix_out = map_one - lambda_now * map_two
    mix_out = (
        mix_out
        * lax.rsqrt(jnp.mean(mix_out * mix_out, axis=2, keepdims=True) + 1e-05)
        * subln_gain
        * (1.0 - LAMBDA_BASE)
    )
    return mix_out.astype(jnp.bfloat16).reshape(row_count, head_count * value_width)


def mlp_gather(block, axis_size):
    index = lax.axis_index("mlp")
    pieces = [block]
    for shift in range(1, axis_size):
        pieces.append(
            lax.ppermute(block, "mlp", [(i, (i + shift) % axis_size) for i in range(axis_size)])
        )
    stacked = jnp.stack(pieces, axis=0)
    source_of = (index - jnp.arange(axis_size, dtype=jnp.int32)) % axis_size
    gathered = jnp.take(stacked, source_of, axis=0)
    return jnp.concatenate([gathered[k] for k in range(axis_size)], axis=1)


def down_and_scatter(hidden_act, down_full, axis_size, rows):
    index = lax.axis_index("mlp")

    def block_for(target):
        weight_rows = down_block_rows(down_full, target, rows)
        value = lax.dot_general(
            hidden_act, weight_rows, (((1,), (1,)), ((), ())), preferred_element_type=jnp.float32
        )
        return block_to_req_order(value.astype(jnp.bfloat16), rows)

    incoming = []
    for shift in range(1, axis_size):
        target = (index + shift) % axis_size
        incoming.append(
            lax.ppermute(
                block_for(target), "mlp", [(i, (i + shift) % axis_size) for i in range(axis_size)]
            )
        )
    total = block_for(index).astype(jnp.float32)
    for received in incoming:
        total = total + received.astype(jnp.float32)
    return total


REQ_PARTS = ("x", "z", "c")


def gather_rows(block):
    out = lax.all_gather(block, "x", axis=0, tiled=True)
    out = lax.all_gather(out, "z", axis=0, tiled=True)
    other = lax.ppermute(out, "c", [(0, 1), (1, 0)])
    return jnp.concatenate([out, other], axis=0)


def to_gathered_order(act, rows):
    nx, nz, nc = [lax.axis_size(name) for name in REQ_PARTS]
    n = act.shape[0]
    own = lax.axis_index("c")
    split = act.reshape(n, nx, nz, nc, rows)
    split = jnp.where(own == 0, split, split[:, :, :, ::-1, :])
    return split.transpose(0, 3, 2, 1, 4).reshape(n, -1)


def down_block_rows(down_full, target, rows):
    nx, nz, nc = [lax.axis_size(name) for name in REQ_PARTS]
    split = down_full.reshape(nc, nz, nx, rows, down_full.shape[1])
    picked = lax.dynamic_index_in_dim(split, target, 2, keepdims=False)
    return picked.reshape(nc * nz * rows, down_full.shape[1])


def block_to_req_order(value, rows):
    nx, nz, nc = [lax.axis_size(name) for name in REQ_PARTS]
    n = value.shape[0]
    own = lax.axis_index("c")
    split = value.reshape(n, nc, nz, rows)
    split = jnp.where(own == 0, split, split[:, ::-1, :, :])
    return split.transpose(0, 2, 1, 3).reshape(n, -1)


def per_device(
    queries,
    new_kv,
    cache_pool,
    page_table,
    assignment,
    lengths,
    lambda_vectors,
    subln_gain,
    residual,
    out_weight,
    norm_gain,
    gate_weight,
    up_weight,
    down_weight_t,
):
    widths = [out_weight.shape[1], gate_weight.shape[1], up_weight.shape[1], down_weight_t.shape[1]]
    packed = jnp.concatenate([out_weight, gate_weight, up_weight, down_weight_t], axis=1)
    gathered = gather_rows(packed)
    bounds = [0]
    for w in widths:
        bounds.append(bounds[-1] + w)
    out_full, gate_full, up_full, down_full = [
        gathered[:, bounds[i] : bounds[i + 1]] for i in range(4)
    ]
    attn_out = attend(
        queries, new_kv, cache_pool, page_table, assignment, lengths, lambda_vectors, subln_gain
    )
    mlp_size = D // residual.shape[1]
    heads_all = mlp_gather(attn_out, mlp_size)
    rows = out_weight.shape[0]
    projected = jnp.dot(
        to_gathered_order(heads_all, rows), out_full, preferred_element_type=jnp.float32
    )
    stream = (residual.astype(jnp.float32) + projected).astype(jnp.bfloat16)
    stream_all = mlp_gather(stream, mlp_size).astype(jnp.float32)
    squares = jnp.sum(stream_all * stream_all, axis=1, keepdims=True)
    normed = (stream_all * lax.rsqrt(squares / D + 1e-05) * norm_gain).astype(jnp.bfloat16)
    normed = to_gathered_order(normed, rows)
    gate_value = jnp.dot(normed, gate_full, preferred_element_type=jnp.float32)
    up_value = jnp.dot(normed, up_full, preferred_element_type=jnp.float32)
    hidden_act = (jax.nn.silu(gate_value) * up_value).astype(jnp.bfloat16)
    summed = down_and_scatter(hidden_act, down_full, mlp_size, out_weight.shape[0])
    return (stream.astype(jnp.float32) + summed).astype(jnp.bfloat16)


def solution(mesh):
    split = Mesh(mesh.devices.reshape(4, 16, 2, mesh.devices.shape[1]), REQ_PARTS + ("mlp",))
    req = REQ_PARTS
    in_specs = (
        P(req, "mlp", None),
        P(req, "mlp", None),
        P(req, None, "mlp", None),
        P(req, None),
        P(req),
        P(),
        P(),
        P(),
        P(req, "mlp"),
        P(req, "mlp"),
        P(),
        P(req, "mlp"),
        P(req, "mlp"),
        P(req, "mlp"),
    )
    out_specs = P(req, "mlp")
    return jax.shard_map(
        per_device, mesh=split, in_specs=in_specs, out_specs=out_specs, check_vma=False
    )
```

```python
import jax
import jax.numpy as jnp
from jax import lax
from jax.sharding import Mesh, PartitionSpec as P

D = 2048


NEG_FILL = -1e30
LAMBDA_BASE = 0.2


def attend(
    queries, new_kv, cache_pool, page_table, assignment, lengths, lambda_vectors, subln_gain
):
    row_count, head_count, value_width = queries.shape
    half_size = value_width // 2
    score_scale = half_size ** (-0.5)
    request = assignment[0]
    cached = jnp.sum(
        jnp.where(jnp.arange(lengths.shape[0], dtype=jnp.int32) == request, lengths, 0)
    )
    pages = jnp.take(cache_pool, page_table[0], axis=0)
    cached_rows = pages.reshape(-1, head_count, cache_pool.shape[3])
    cache_len = cached_rows.shape[0]
    key_rows = jnp.concatenate([cached_rows, new_kv], axis=0)
    positions = jnp.arange(cache_len, dtype=jnp.int32)
    token_pos = jnp.arange(row_count, dtype=jnp.int32)
    visible = jnp.concatenate(
        [
            jnp.broadcast_to((positions < cached)[None, :], (row_count, cache_len)),
            token_pos[None, :] <= token_pos[:, None],
        ],
        axis=1,
    )
    value_rows = key_rows[:, :, 2 * half_size :]

    def one_map(query_rows, key_half):
        score = (
            jnp.einsum("nhd,khd->nhk", query_rows, key_half, preferred_element_type=jnp.float32)
            * score_scale
        )
        score = jnp.where(visible[:, None, :], score, NEG_FILL)
        row_max = jnp.max(score, axis=2, keepdims=True)
        exp_terms = jnp.where(visible[:, None, :], jnp.exp(score - row_max), 0.0)
        exp_total = jnp.sum(exp_terms, axis=2)
        mixed = jnp.einsum(
            "nhk,khd->nhd",
            exp_terms.astype(jnp.bfloat16),
            value_rows,
            preferred_element_type=jnp.float32,
        )
        return mixed / exp_total[:, :, None]

    map_one = one_map(queries[:, :, :half_size], key_rows[:, :, :half_size])
    map_two = one_map(queries[:, :, half_size:], key_rows[:, :, half_size : 2 * half_size])
    lambda_now = (
        jnp.exp(jnp.sum(lambda_vectors[0] * lambda_vectors[1]))
        - jnp.exp(jnp.sum(lambda_vectors[2] * lambda_vectors[3]))
        + LAMBDA_BASE
    )
    mix_out = map_one - lambda_now * map_two
    mix_out = (
        mix_out
        * lax.rsqrt(jnp.mean(mix_out * mix_out, axis=2, keepdims=True) + 1e-05)
        * subln_gain
        * (1.0 - LAMBDA_BASE)
    )
    return mix_out.astype(jnp.bfloat16).reshape(row_count, head_count * value_width)


def mlp_gather(block, axis_size):
    index = lax.axis_index("mlp")
    pieces = [block]
    for shift in range(1, axis_size):
        pieces.append(
            lax.ppermute(block, "mlp", [(i, (i + shift) % axis_size) for i in range(axis_size)])
        )
    stacked = jnp.stack(pieces, axis=0)
    source_of = (index - jnp.arange(axis_size, dtype=jnp.int32)) % axis_size
    gathered = jnp.take(stacked, source_of, axis=0)
    return jnp.concatenate([gathered[k] for k in range(axis_size)], axis=1)


def down_and_scatter(hidden_act, down_full, axis_size, rows):
    index = lax.axis_index("mlp")

    def block_for(target):
        weight_rows = down_block_rows(down_full, target, rows)
        value = lax.dot_general(
            hidden_act, weight_rows, (((1,), (1,)), ((), ())), preferred_element_type=jnp.float32
        )
        return block_to_req_order(value.astype(jnp.bfloat16), rows)

    incoming = []
    for shift in range(1, axis_size):
        target = (index + shift) % axis_size
        incoming.append(
            lax.ppermute(
                block_for(target), "mlp", [(i, (i + shift) % axis_size) for i in range(axis_size)]
            )
        )
    total = block_for(index).astype(jnp.float32)
    for received in incoming:
        total = total + received.astype(jnp.float32)
    return total


REQ_PARTS = ("x", "z", "c")


def gather_over_xz(block):
    out = lax.all_gather(block, "x", axis=0, tiled=True)
    return lax.all_gather(out, "z", axis=0, tiled=True)


def swap_with_core(rows_xz):
    other = lax.ppermute(rows_xz, "c", [(0, 1), (1, 0)])
    return jnp.concatenate([rows_xz, other], axis=0)


def to_gathered_order(act, rows):
    nx, nz, nc = [lax.axis_size(name) for name in REQ_PARTS]
    n = act.shape[0]
    own = lax.axis_index("c")
    split = act.reshape(n, nx, nz, nc, rows)
    split = jnp.where(own == 0, split, split[:, :, :, ::-1, :])
    return split.transpose(0, 3, 2, 1, 4).reshape(n, -1)


def down_block_rows(down_full, target, rows):
    nx, nz, nc = [lax.axis_size(name) for name in REQ_PARTS]
    split = down_full.reshape(nc, nz, nx, rows, down_full.shape[1])
    picked = lax.dynamic_index_in_dim(split, target, 2, keepdims=False)
    return picked.reshape(nc * nz * rows, down_full.shape[1])


def block_to_req_order(value, rows):
    nx, nz, nc = [lax.axis_size(name) for name in REQ_PARTS]
    n = value.shape[0]
    own = lax.axis_index("c")
    split = value.reshape(n, nc, nz, rows)
    split = jnp.where(own == 0, split, split[:, ::-1, :, :])
    return split.transpose(0, 2, 1, 3).reshape(n, -1)


def per_device(
    queries,
    new_kv,
    cache_pool,
    page_table,
    assignment,
    lengths,
    lambda_vectors,
    subln_gain,
    residual,
    out_weight,
    norm_gain,
    gate_weight,
    up_weight,
    down_weight_t,
):
    widths = [out_weight.shape[1], gate_weight.shape[1], up_weight.shape[1], down_weight_t.shape[1]]
    packed = jnp.concatenate([out_weight, gate_weight, up_weight, down_weight_t], axis=1)
    rows_xz = gather_over_xz(packed)
    attn_out = attend(
        queries, new_kv, cache_pool, page_table, assignment, lengths, lambda_vectors, subln_gain
    )
    mlp_size = D // residual.shape[1]
    heads_all = mlp_gather(attn_out, mlp_size)
    rows_xz, heads_all = lax.optimization_barrier((rows_xz, heads_all))
    gathered = swap_with_core(rows_xz)
    bounds = [0]
    for w in widths:
        bounds.append(bounds[-1] + w)
    out_full, gate_full, up_full, down_full = [
        gathered[:, bounds[i] : bounds[i + 1]] for i in range(4)
    ]
    rows = out_weight.shape[0]
    projected = jnp.dot(
        to_gathered_order(heads_all, rows), out_full, preferred_element_type=jnp.float32
    )
    stream = (residual.astype(jnp.float32) + projected).astype(jnp.bfloat16)
    stream_all = mlp_gather(stream, mlp_size).astype(jnp.float32)
    squares = jnp.sum(stream_all * stream_all, axis=1, keepdims=True)
    normed = (stream_all * lax.rsqrt(squares / D + 1e-05) * norm_gain).astype(jnp.bfloat16)
    normed = to_gathered_order(normed, rows)
    gate_value = jnp.dot(normed, gate_full, preferred_element_type=jnp.float32)
    up_value = jnp.dot(normed, up_full, preferred_element_type=jnp.float32)
    hidden_act = (jax.nn.silu(gate_value) * up_value).astype(jnp.bfloat16)
    summed = down_and_scatter(hidden_act, down_full, mlp_size, out_weight.shape[0])
    return (stream.astype(jnp.float32) + summed).astype(jnp.bfloat16)


def solution(mesh):
    split = Mesh(mesh.devices.reshape(4, 16, 2, mesh.devices.shape[1]), REQ_PARTS + ("mlp",))
    req = REQ_PARTS
    in_specs = (
        P(req, "mlp", None),
        P(req, "mlp", None),
        P(req, None, "mlp", None),
        P(req, None),
        P(req),
        P(),
        P(),
        P(),
        P(req, "mlp"),
        P(req, "mlp"),
        P(),
        P(req, "mlp"),
        P(req, "mlp"),
        P(req, "mlp"),
    )
    out_specs = P(req, "mlp")
    return jax.shard_map(
        per_device, mesh=split, in_specs=in_specs, out_specs=out_specs, check_vma=False
    )
```

```python
import jax
import jax.numpy as jnp
from jax import lax
from jax.sharding import Mesh, PartitionSpec as P

D = 2048


NEG_FILL = -1e30
LAMBDA_BASE = 0.2


def attend(
    queries, new_kv, cache_pool, page_table, assignment, lengths, lambda_vectors, subln_gain
):
    row_count, head_count, value_width = queries.shape
    half_size = value_width // 2
    score_scale = half_size ** (-0.5)
    request = assignment[0]
    cached = jnp.sum(
        jnp.where(jnp.arange(lengths.shape[0], dtype=jnp.int32) == request, lengths, 0)
    )
    pages = jnp.take(cache_pool, page_table[0], axis=0)
    cached_rows = pages.reshape(-1, head_count, cache_pool.shape[3])
    cache_len = cached_rows.shape[0]
    key_rows = jnp.concatenate([cached_rows, new_kv], axis=0)
    positions = jnp.arange(cache_len, dtype=jnp.int32)
    token_pos = jnp.arange(row_count, dtype=jnp.int32)
    visible = jnp.concatenate(
        [
            jnp.broadcast_to((positions < cached)[None, :], (row_count, cache_len)),
            token_pos[None, :] <= token_pos[:, None],
        ],
        axis=1,
    )
    value_rows = key_rows[:, :, 2 * half_size :]

    def one_map(query_rows, key_half):
        score = (
            jnp.einsum("nhd,khd->nhk", query_rows, key_half, preferred_element_type=jnp.float32)
            * score_scale
        )
        score = jnp.where(visible[:, None, :], score, NEG_FILL)
        row_max = jnp.max(score, axis=2, keepdims=True)
        exp_terms = jnp.where(visible[:, None, :], jnp.exp(score - row_max), 0.0)
        exp_total = jnp.sum(exp_terms, axis=2)
        mixed = jnp.einsum(
            "nhk,khd->nhd",
            exp_terms.astype(jnp.bfloat16),
            value_rows,
            preferred_element_type=jnp.float32,
        )
        return mixed / exp_total[:, :, None]

    map_one = one_map(queries[:, :, :half_size], key_rows[:, :, :half_size])
    map_two = one_map(queries[:, :, half_size:], key_rows[:, :, half_size : 2 * half_size])
    lambda_now = (
        jnp.exp(jnp.sum(lambda_vectors[0] * lambda_vectors[1]))
        - jnp.exp(jnp.sum(lambda_vectors[2] * lambda_vectors[3]))
        + LAMBDA_BASE
    )
    mix_out = map_one - lambda_now * map_two
    mix_out = (
        mix_out
        * lax.rsqrt(jnp.mean(mix_out * mix_out, axis=2, keepdims=True) + 1e-05)
        * subln_gain
        * (1.0 - LAMBDA_BASE)
    )
    return mix_out.astype(jnp.bfloat16).reshape(row_count, head_count * value_width)


def mlp_gather(block, axis_size):
    index = lax.axis_index("mlp")
    pieces = [block]
    for shift in range(1, axis_size):
        pieces.append(
            lax.ppermute(block, "mlp", [(i, (i + shift) % axis_size) for i in range(axis_size)])
        )
    stacked = jnp.stack(pieces, axis=0)
    source_of = (index - jnp.arange(axis_size, dtype=jnp.int32)) % axis_size
    gathered = jnp.take(stacked, source_of, axis=0)
    return jnp.concatenate([gathered[k] for k in range(axis_size)], axis=1)


def down_and_scatter(hidden_act, down_full, axis_size, rows):
    index = lax.axis_index("mlp")

    def block_for(target):
        weight_rows = down_block_rows(down_full, target, rows)
        value = lax.dot_general(
            hidden_act, weight_rows, (((1,), (1,)), ((), ())), preferred_element_type=jnp.float32
        )
        return block_to_req_order(value.astype(jnp.bfloat16), rows)

    incoming = []
    for shift in range(1, axis_size):
        target = (index + shift) % axis_size
        incoming.append(
            lax.ppermute(
                block_for(target), "mlp", [(i, (i + shift) % axis_size) for i in range(axis_size)]
            )
        )
    total = block_for(index).astype(jnp.float32)
    for received in incoming:
        total = total + received.astype(jnp.float32)
    return total


REQ_PARTS = ("x", "z", "c")


def gather_over_xz(block):
    out = lax.all_gather(block, "x", axis=0, tiled=True)
    return lax.all_gather(out, "z", axis=0, tiled=True)


def swap_with_core(rows_xz):
    return [rows_xz, lax.ppermute(rows_xz, "c", [(0, 1), (1, 0)])]


def split_dot(act, halves):
    size = halves[0].shape[0]
    total = None
    for j, half in enumerate(halves):
        part = jnp.dot(act[:, j * size : (j + 1) * size], half, preferred_element_type=jnp.float32)
        total = part if total is None else total + part
    return total


def to_gathered_order(act, rows):
    nx, nz, nc = [lax.axis_size(name) for name in REQ_PARTS]
    n = act.shape[0]
    own = lax.axis_index("c")
    split = act.reshape(n, nx, nz, nc, rows)
    split = jnp.where(own == 0, split, split[:, :, :, ::-1, :])
    return split.transpose(0, 3, 2, 1, 4).reshape(n, -1)


def down_block_rows(down_halves, target, rows):
    nx, nz, nc = [lax.axis_size(name) for name in REQ_PARTS]
    picked = []
    for half in down_halves:
        split = half.reshape(nz, nx, rows, half.shape[1])
        one = lax.dynamic_index_in_dim(split, target, 1, keepdims=False)
        picked.append(one.reshape(nz * rows, half.shape[1]))
    return jnp.concatenate(picked, axis=0)


def block_to_req_order(value, rows):
    nx, nz, nc = [lax.axis_size(name) for name in REQ_PARTS]
    n = value.shape[0]
    own = lax.axis_index("c")
    split = value.reshape(n, nc, nz, rows)
    split = jnp.where(own == 0, split, split[:, ::-1, :, :])
    return split.transpose(0, 2, 1, 3).reshape(n, -1)


def per_device(
    queries,
    new_kv,
    cache_pool,
    page_table,
    assignment,
    lengths,
    lambda_vectors,
    subln_gain,
    residual,
    out_weight,
    norm_gain,
    gate_weight,
    up_weight,
    down_weight_t,
):
    widths = [out_weight.shape[1], gate_weight.shape[1], up_weight.shape[1], down_weight_t.shape[1]]
    packed = jnp.concatenate([out_weight, gate_weight, up_weight, down_weight_t], axis=1)
    rows_xz = gather_over_xz(packed)
    attn_out = attend(
        queries, new_kv, cache_pool, page_table, assignment, lengths, lambda_vectors, subln_gain
    )
    mlp_size = D // residual.shape[1]
    heads_all = mlp_gather(attn_out, mlp_size)
    rows_xz, heads_all = lax.optimization_barrier((rows_xz, heads_all))
    halves = swap_with_core(rows_xz)
    bounds = [0]
    for w in widths:
        bounds.append(bounds[-1] + w)
    out_full, gate_full, up_full, down_full = [
        [half[:, bounds[i] : bounds[i + 1]] for half in halves] for i in range(4)
    ]
    rows = out_weight.shape[0]
    projected = split_dot(to_gathered_order(heads_all, rows), out_full)
    stream = (residual.astype(jnp.float32) + projected).astype(jnp.bfloat16)
    stream_all = mlp_gather(stream, mlp_size).astype(jnp.float32)
    squares = jnp.sum(stream_all * stream_all, axis=1, keepdims=True)
    normed = (stream_all * lax.rsqrt(squares / D + 1e-05) * norm_gain).astype(jnp.bfloat16)
    normed = to_gathered_order(normed, rows)
    gate_value = split_dot(normed, gate_full)
    up_value = split_dot(normed, up_full)
    hidden_act = (jax.nn.silu(gate_value) * up_value).astype(jnp.bfloat16)
    summed = down_and_scatter(hidden_act, down_full, mlp_size, out_weight.shape[0])
    return (stream.astype(jnp.float32) + summed).astype(jnp.bfloat16)


def solution(mesh):
    split = Mesh(mesh.devices.reshape(4, 16, 2, mesh.devices.shape[1]), REQ_PARTS + ("mlp",))
    req = REQ_PARTS
    in_specs = (
        P(req, "mlp", None),
        P(req, "mlp", None),
        P(req, None, "mlp", None),
        P(req, None),
        P(req),
        P(),
        P(),
        P(),
        P(req, "mlp"),
        P(req, "mlp"),
        P(),
        P(req, "mlp"),
        P(req, "mlp"),
        P(req, "mlp"),
    )
    out_specs = P(req, "mlp")
    return jax.shard_map(
        per_device, mesh=split, in_specs=in_specs, out_specs=out_specs, check_vma=False
    )
```

```python
import jax
import jax.numpy as jnp
from jax import lax
from jax.sharding import Mesh, PartitionSpec as P

D = 2048


NEG_FILL = -1e30
LAMBDA_BASE = 0.2


def attend(
    queries, new_kv, cache_pool, page_table, assignment, lengths, lambda_vectors, subln_gain
):
    row_count, head_count, value_width = queries.shape
    half_size = value_width // 2
    score_scale = half_size ** (-0.5)
    request = assignment[0]
    cached = jnp.sum(
        jnp.where(jnp.arange(lengths.shape[0], dtype=jnp.int32) == request, lengths, 0)
    )
    pages = jnp.take(cache_pool, page_table[0], axis=0)
    cached_rows = pages.reshape(-1, head_count, cache_pool.shape[3])
    cache_len = cached_rows.shape[0]
    key_rows = jnp.concatenate([cached_rows, new_kv], axis=0)
    positions = jnp.arange(cache_len, dtype=jnp.int32)
    token_pos = jnp.arange(row_count, dtype=jnp.int32)
    visible = jnp.concatenate(
        [
            jnp.broadcast_to((positions < cached)[None, :], (row_count, cache_len)),
            token_pos[None, :] <= token_pos[:, None],
        ],
        axis=1,
    )
    value_rows = key_rows[:, :, 2 * half_size :]

    def one_map(query_rows, key_half):
        score = (
            jnp.einsum("nhd,khd->nhk", query_rows, key_half, preferred_element_type=jnp.float32)
            * score_scale
        )
        score = jnp.where(visible[:, None, :], score, NEG_FILL)
        row_max = jnp.max(score, axis=2, keepdims=True)
        exp_terms = jnp.where(visible[:, None, :], jnp.exp(score - row_max), 0.0)
        exp_total = jnp.sum(exp_terms, axis=2)
        mixed = jnp.einsum(
            "nhk,khd->nhd",
            exp_terms.astype(jnp.bfloat16),
            value_rows,
            preferred_element_type=jnp.float32,
        )
        return mixed / exp_total[:, :, None]

    map_one = one_map(queries[:, :, :half_size], key_rows[:, :, :half_size])
    map_two = one_map(queries[:, :, half_size:], key_rows[:, :, half_size : 2 * half_size])
    lambda_now = (
        jnp.exp(jnp.sum(lambda_vectors[0] * lambda_vectors[1]))
        - jnp.exp(jnp.sum(lambda_vectors[2] * lambda_vectors[3]))
        + LAMBDA_BASE
    )
    mix_out = map_one - lambda_now * map_two
    mix_out = (
        mix_out
        * lax.rsqrt(jnp.mean(mix_out * mix_out, axis=2, keepdims=True) + 1e-05)
        * subln_gain
        * (1.0 - LAMBDA_BASE)
    )
    return mix_out.astype(jnp.bfloat16).reshape(row_count, head_count * value_width)


def mlp_gather(block, axis_size):
    index = lax.axis_index("mlp")
    pieces = [block]
    for shift in range(1, axis_size):
        pieces.append(
            lax.ppermute(block, "mlp", [(i, (i + shift) % axis_size) for i in range(axis_size)])
        )
    stacked = jnp.stack(pieces, axis=0)
    source_of = (index - jnp.arange(axis_size, dtype=jnp.int32)) % axis_size
    gathered = jnp.take(stacked, source_of, axis=0)
    return jnp.concatenate([gathered[k] for k in range(axis_size)], axis=1)


def down_and_scatter(hidden_act, down_full, axis_size, rows):
    index = lax.axis_index("mlp")

    def block_for(target):
        weight_rows = down_block_rows(down_full, target, rows)
        value = lax.dot_general(
            hidden_act, weight_rows, (((1,), (1,)), ((), ())), preferred_element_type=jnp.float32
        )
        return block_to_req_order(value.astype(jnp.bfloat16), rows)

    incoming = []
    for shift in range(1, axis_size):
        target = (index + shift) % axis_size
        incoming.append(
            lax.ppermute(
                block_for(target), "mlp", [(i, (i + shift) % axis_size) for i in range(axis_size)]
            )
        )
    total = block_for(index).astype(jnp.float32)
    for received in incoming:
        total = total + received.astype(jnp.float32)
    return total


REQ_PARTS = ("x", "z", "c")


def gather_over_xz(block):
    size = lax.axis_size("x")
    index = lax.axis_index("x")
    out = block
    bit = 1
    while bit < size:
        partner = lax.ppermute(out, "x", [(i, i ^ bit) for i in range(size)])
        out = jnp.where(
            (index & bit) == 0,
            jnp.concatenate([out, partner], axis=0),
            jnp.concatenate([partner, out], axis=0),
        )
        bit *= 2
    return lax.all_gather(out, "z", axis=0, tiled=True)


def swap_with_core(rows_xz):
    return [rows_xz, lax.ppermute(rows_xz, "c", [(0, 1), (1, 0)])]


def split_dot(act, halves):
    size = halves[0].shape[0]
    total = None
    for j, half in enumerate(halves):
        part = jnp.dot(act[:, j * size : (j + 1) * size], half, preferred_element_type=jnp.float32)
        total = part if total is None else total + part
    return total


def to_gathered_order(act, rows):
    nx, nz, nc = [lax.axis_size(name) for name in REQ_PARTS]
    n = act.shape[0]
    own = lax.axis_index("c")
    split = act.reshape(n, nx, nz, nc, rows)
    split = jnp.where(own == 0, split, split[:, :, :, ::-1, :])
    return split.transpose(0, 3, 2, 1, 4).reshape(n, -1)


def down_block_rows(down_halves, target, rows):
    nx, nz, nc = [lax.axis_size(name) for name in REQ_PARTS]
    picked = []
    for half in down_halves:
        split = half.reshape(nz, nx, rows, half.shape[1])
        one = lax.dynamic_index_in_dim(split, target, 1, keepdims=False)
        picked.append(one.reshape(nz * rows, half.shape[1]))
    return jnp.concatenate(picked, axis=0)


def block_to_req_order(value, rows):
    nx, nz, nc = [lax.axis_size(name) for name in REQ_PARTS]
    n = value.shape[0]
    own = lax.axis_index("c")
    split = value.reshape(n, nc, nz, rows)
    split = jnp.where(own == 0, split, split[:, ::-1, :, :])
    return split.transpose(0, 2, 1, 3).reshape(n, -1)


def per_device(
    queries,
    new_kv,
    cache_pool,
    page_table,
    assignment,
    lengths,
    lambda_vectors,
    subln_gain,
    residual,
    out_weight,
    norm_gain,
    gate_weight,
    up_weight,
    down_weight_t,
):
    widths = [out_weight.shape[1], gate_weight.shape[1], up_weight.shape[1], down_weight_t.shape[1]]
    packed = jnp.concatenate([out_weight, gate_weight, up_weight, down_weight_t], axis=1)
    rows_xz = gather_over_xz(packed)
    attn_out = attend(
        queries, new_kv, cache_pool, page_table, assignment, lengths, lambda_vectors, subln_gain
    )
    mlp_size = D // residual.shape[1]
    heads_all = mlp_gather(attn_out, mlp_size)
    rows_xz, heads_all = lax.optimization_barrier((rows_xz, heads_all))
    halves = swap_with_core(rows_xz)
    bounds = [0]
    for w in widths:
        bounds.append(bounds[-1] + w)
    out_full, gate_full, up_full, down_full = [
        [half[:, bounds[i] : bounds[i + 1]] for half in halves] for i in range(4)
    ]
    rows = out_weight.shape[0]
    projected = split_dot(to_gathered_order(heads_all, rows), out_full)
    stream = (residual.astype(jnp.float32) + projected).astype(jnp.bfloat16)
    stream_all = mlp_gather(stream, mlp_size).astype(jnp.float32)
    squares = jnp.sum(stream_all * stream_all, axis=1, keepdims=True)
    normed = (stream_all * lax.rsqrt(squares / D + 1e-05) * norm_gain).astype(jnp.bfloat16)
    normed = to_gathered_order(normed, rows)
    gate_value = split_dot(normed, gate_full)
    up_value = split_dot(normed, up_full)
    hidden_act = (jax.nn.silu(gate_value) * up_value).astype(jnp.bfloat16)
    summed = down_and_scatter(hidden_act, down_full, mlp_size, out_weight.shape[0])
    return (stream.astype(jnp.float32) + summed).astype(jnp.bfloat16)


def solution(mesh):
    split = Mesh(mesh.devices.reshape(4, 16, 2, mesh.devices.shape[1]), REQ_PARTS + ("mlp",))
    req = REQ_PARTS
    in_specs = (
        P(req, "mlp", None),
        P(req, "mlp", None),
        P(req, None, "mlp", None),
        P(req, None),
        P(req),
        P(),
        P(),
        P(),
        P(req, "mlp"),
        P(req, "mlp"),
        P(),
        P(req, "mlp"),
        P(req, "mlp"),
        P(req, "mlp"),
    )
    out_specs = P(req, "mlp")
    return jax.shard_map(
        per_device, mesh=split, in_specs=in_specs, out_specs=out_specs, check_vma=False
    )
```

```python
import jax
import jax.numpy as jnp
from jax import lax
from jax.sharding import Mesh, PartitionSpec as P

D = 2048


NEG_FILL = -1e30
LAMBDA_BASE = 0.2


def attend(
    queries, new_kv, cache_pool, page_table, assignment, lengths, lambda_vectors, subln_gain
):
    row_count, head_count, value_width = queries.shape
    half_size = value_width // 2
    score_scale = half_size ** (-0.5)
    request = assignment[0]
    cached = jnp.sum(
        jnp.where(jnp.arange(lengths.shape[0], dtype=jnp.int32) == request, lengths, 0)
    )
    pages = jnp.take(cache_pool, page_table[0], axis=0)
    cached_rows = pages.reshape(-1, head_count, cache_pool.shape[3])
    cache_len = cached_rows.shape[0]
    key_rows = jnp.concatenate([cached_rows, new_kv], axis=0)
    positions = jnp.arange(cache_len, dtype=jnp.int32)
    token_pos = jnp.arange(row_count, dtype=jnp.int32)
    visible = jnp.concatenate(
        [
            jnp.broadcast_to((positions < cached)[None, :], (row_count, cache_len)),
            token_pos[None, :] <= token_pos[:, None],
        ],
        axis=1,
    )
    value_rows = key_rows[:, :, 2 * half_size :]

    def one_map(query_rows, key_half):
        score = (
            jnp.einsum("nhd,khd->nhk", query_rows, key_half, preferred_element_type=jnp.float32)
            * score_scale
        )
        score = jnp.where(visible[:, None, :], score, NEG_FILL)
        row_max = jnp.max(score, axis=2, keepdims=True)
        exp_terms = jnp.where(visible[:, None, :], jnp.exp(score - row_max), 0.0)
        exp_total = jnp.sum(exp_terms, axis=2)
        mixed = jnp.einsum(
            "nhk,khd->nhd",
            exp_terms.astype(jnp.bfloat16),
            value_rows,
            preferred_element_type=jnp.float32,
        )
        return mixed / exp_total[:, :, None]

    map_one = one_map(queries[:, :, :half_size], key_rows[:, :, :half_size])
    map_two = one_map(queries[:, :, half_size:], key_rows[:, :, half_size : 2 * half_size])
    lambda_now = (
        jnp.exp(jnp.sum(lambda_vectors[0] * lambda_vectors[1]))
        - jnp.exp(jnp.sum(lambda_vectors[2] * lambda_vectors[3]))
        + LAMBDA_BASE
    )
    mix_out = map_one - lambda_now * map_two
    mix_out = (
        mix_out
        * lax.rsqrt(jnp.mean(mix_out * mix_out, axis=2, keepdims=True) + 1e-05)
        * subln_gain
        * (1.0 - LAMBDA_BASE)
    )
    return mix_out.astype(jnp.bfloat16).reshape(row_count, head_count * value_width)


def mlp_gather(block, axis_size):
    index = lax.axis_index("mlp")
    pieces = [block]
    for shift in range(1, axis_size):
        pieces.append(
            lax.ppermute(block, "mlp", [(i, (i + shift) % axis_size) for i in range(axis_size)])
        )
    stacked = jnp.stack(pieces, axis=0)
    source_of = (index - jnp.arange(axis_size, dtype=jnp.int32)) % axis_size
    gathered = jnp.take(stacked, source_of, axis=0)
    return jnp.concatenate([gathered[k] for k in range(axis_size)], axis=1)


def down_and_scatter(hidden_act, down_halves, axis_size, rows):
    index = lax.axis_index("mlp")
    nx, nz, nc = [lax.axis_size(name) for name in REQ_PARTS]
    n = hidden_act.shape[0]
    own = lax.axis_index("c")
    parts = []
    for half in down_halves:
        value = lax.dot_general(
            hidden_act, half, (((1,), (1,)), ((), ())), preferred_element_type=jnp.float32
        )
        parts.append(value.astype(jnp.bfloat16).reshape(n, nz, nx, rows))
    both = jnp.stack(parts, axis=1)
    both = jnp.where(own == 0, both, both[:, ::-1])

    def block_for(target):
        picked = lax.dynamic_index_in_dim(both, target, 3, keepdims=False)
        return picked.transpose(0, 2, 1, 3).reshape(n, -1)

    incoming = []
    for shift in range(1, axis_size):
        target = (index + shift) % axis_size
        incoming.append(
            lax.ppermute(
                block_for(target), "mlp", [(i, (i + shift) % axis_size) for i in range(axis_size)]
            )
        )
    total = block_for(index).astype(jnp.float32)
    for received in incoming:
        total = total + received.astype(jnp.float32)
    return total


REQ_PARTS = ("x", "z", "c")


def gather_over_xz(block):
    out = lax.all_gather(block, "x", axis=0, tiled=True)
    return lax.all_gather(out, "z", axis=0, tiled=True)


def swap_with_core(rows_xz):
    return [rows_xz, lax.ppermute(rows_xz, "c", [(0, 1), (1, 0)])]


def split_dot(act, halves):
    size = halves[0].shape[0]
    total = None
    for j, half in enumerate(halves):
        part = jnp.dot(act[:, j * size : (j + 1) * size], half, preferred_element_type=jnp.float32)
        total = part if total is None else total + part
    return total


def to_gathered_order(act, rows):
    nx, nz, nc = [lax.axis_size(name) for name in REQ_PARTS]
    n = act.shape[0]
    own = lax.axis_index("c")
    split = act.reshape(n, nx, nz, nc, rows)
    split = jnp.where(own == 0, split, split[:, :, :, ::-1, :])
    return split.transpose(0, 3, 2, 1, 4).reshape(n, -1)


def per_device(
    queries,
    new_kv,
    cache_pool,
    page_table,
    assignment,
    lengths,
    lambda_vectors,
    subln_gain,
    residual,
    out_weight,
    norm_gain,
    gate_weight,
    up_weight,
    down_weight_t,
):
    widths = [out_weight.shape[1], gate_weight.shape[1], up_weight.shape[1], down_weight_t.shape[1]]
    packed = jnp.concatenate([out_weight, gate_weight, up_weight, down_weight_t], axis=1)
    rows_xz = gather_over_xz(packed)
    attn_out = attend(
        queries, new_kv, cache_pool, page_table, assignment, lengths, lambda_vectors, subln_gain
    )
    mlp_size = D // residual.shape[1]
    heads_all = mlp_gather(attn_out, mlp_size)
    rows_xz, heads_all = lax.optimization_barrier((rows_xz, heads_all))
    halves = swap_with_core(rows_xz)
    bounds = [0]
    for w in widths:
        bounds.append(bounds[-1] + w)
    out_full, gate_full, up_full, down_full = [
        [half[:, bounds[i] : bounds[i + 1]] for half in halves] for i in range(4)
    ]
    rows = out_weight.shape[0]
    projected = split_dot(to_gathered_order(heads_all, rows), out_full)
    stream = (residual.astype(jnp.float32) + projected).astype(jnp.bfloat16)
    stream_all = mlp_gather(stream, mlp_size).astype(jnp.float32)
    squares = jnp.sum(stream_all * stream_all, axis=1, keepdims=True)
    normed = (stream_all * lax.rsqrt(squares / D + 1e-05) * norm_gain).astype(jnp.bfloat16)
    normed = to_gathered_order(normed, rows)
    gate_value = split_dot(normed, gate_full)
    up_value = split_dot(normed, up_full)
    hidden_act = (jax.nn.silu(gate_value) * up_value).astype(jnp.bfloat16)
    summed = down_and_scatter(hidden_act, down_full, mlp_size, out_weight.shape[0])
    return (stream.astype(jnp.float32) + summed).astype(jnp.bfloat16)


def solution(mesh):
    split = Mesh(mesh.devices.reshape(4, 16, 2, mesh.devices.shape[1]), REQ_PARTS + ("mlp",))
    req = REQ_PARTS
    in_specs = (
        P(req, "mlp", None),
        P(req, "mlp", None),
        P(req, None, "mlp", None),
        P(req, None),
        P(req),
        P(),
        P(),
        P(),
        P(req, "mlp"),
        P(req, "mlp"),
        P(),
        P(req, "mlp"),
        P(req, "mlp"),
        P(req, "mlp"),
    )
    out_specs = P(req, "mlp")
    return jax.shard_map(
        per_device, mesh=split, in_specs=in_specs, out_specs=out_specs, check_vma=False
    )
```

```python
import jax
import jax.numpy as jnp
from jax import lax
from jax.sharding import Mesh, PartitionSpec as P

D = 2048


NEG_FILL = -1e30
LAMBDA_BASE = 0.2


def attend(
    queries, new_kv, cache_pool, page_table, assignment, lengths, lambda_vectors, subln_gain
):
    row_count, head_count, value_width = queries.shape
    half_size = value_width // 2
    score_scale = half_size ** (-0.5)
    request = assignment[0]
    cached = jnp.sum(
        jnp.where(jnp.arange(lengths.shape[0], dtype=jnp.int32) == request, lengths, 0)
    )
    pages = jnp.take(cache_pool, page_table[0], axis=0)
    cached_rows = pages.reshape(-1, head_count, cache_pool.shape[3])
    cache_len = cached_rows.shape[0]
    key_rows = jnp.concatenate([cached_rows, new_kv], axis=0)
    positions = jnp.arange(cache_len, dtype=jnp.int32)
    token_pos = jnp.arange(row_count, dtype=jnp.int32)
    visible = jnp.concatenate(
        [
            jnp.broadcast_to((positions < cached)[None, :], (row_count, cache_len)),
            token_pos[None, :] <= token_pos[:, None],
        ],
        axis=1,
    )
    value_rows = key_rows[:, :, 2 * half_size :]

    def one_map(query_rows, key_half):
        score = (
            jnp.einsum("nhd,khd->nhk", query_rows, key_half, preferred_element_type=jnp.float32)
            * score_scale
        )
        score = jnp.where(visible[:, None, :], score, NEG_FILL)
        row_max = jnp.max(score, axis=2, keepdims=True)
        exp_terms = jnp.where(visible[:, None, :], jnp.exp(score - row_max), 0.0)
        exp_total = jnp.sum(exp_terms, axis=2)
        mixed = jnp.einsum(
            "nhk,khd->nhd",
            exp_terms.astype(jnp.bfloat16),
            value_rows,
            preferred_element_type=jnp.float32,
        )
        return mixed / exp_total[:, :, None]

    map_one = one_map(queries[:, :, :half_size], key_rows[:, :, :half_size])
    map_two = one_map(queries[:, :, half_size:], key_rows[:, :, half_size : 2 * half_size])
    lambda_now = (
        jnp.exp(jnp.sum(lambda_vectors[0] * lambda_vectors[1]))
        - jnp.exp(jnp.sum(lambda_vectors[2] * lambda_vectors[3]))
        + LAMBDA_BASE
    )
    mix_out = map_one - lambda_now * map_two
    mix_out = (
        mix_out
        * lax.rsqrt(jnp.mean(mix_out * mix_out, axis=2, keepdims=True) + 1e-05)
        * subln_gain
        * (1.0 - LAMBDA_BASE)
    )
    return mix_out.astype(jnp.bfloat16).reshape(row_count, head_count * value_width)


def mlp_gather(block, axis_size):
    index = lax.axis_index("mlp")
    pieces = [block]
    for shift in range(1, axis_size):
        pieces.append(
            lax.ppermute(block, "mlp", [(i, (i + shift) % axis_size) for i in range(axis_size)])
        )
    stacked = jnp.stack(pieces, axis=0)
    source_of = (index - jnp.arange(axis_size, dtype=jnp.int32)) % axis_size
    gathered = jnp.take(stacked, source_of, axis=0)
    return jnp.concatenate([gathered[k] for k in range(axis_size)], axis=1)


def down_and_scatter(hidden_act, down_halves, axis_size, rows):
    index = lax.axis_index("mlp")
    nx, nz, nc = [lax.axis_size(name) for name in REQ_PARTS]
    n = hidden_act.shape[0]
    own = lax.axis_index("c")
    parts = []
    for half in down_halves:
        value = lax.dot_general(
            hidden_act, half, (((1,), (1,)), ((), ())), preferred_element_type=jnp.float32
        )
        parts.append(value.astype(jnp.bfloat16).reshape(n, nz, nx, rows))
    both = jnp.stack(parts, axis=1)
    both = jnp.where(own == 0, both, both[:, ::-1])

    def block_for(target):
        picked = lax.dynamic_index_in_dim(both, target, 3, keepdims=False)
        return picked.transpose(0, 2, 1, 3).reshape(n, -1)

    incoming = []
    for shift in range(1, axis_size):
        target = (index + shift) % axis_size
        incoming.append(
            lax.ppermute(
                block_for(target), "mlp", [(i, (i + shift) % axis_size) for i in range(axis_size)]
            )
        )
    total = block_for(index).astype(jnp.float32)
    for received in incoming:
        total = total + received.astype(jnp.float32)
    return total


REQ_PARTS = ("x", "z", "c")


def gather_over_xz(block):
    out = lax.all_gather(block, "x", axis=0, tiled=True)
    return lax.all_gather(out, "z", axis=0, tiled=True)


def swap_with_core(rows_xz):
    return [rows_xz, lax.ppermute(rows_xz, "c", [(0, 1), (1, 0)])]


def split_dot(act, halves):
    size = halves[0].shape[0]
    total = None
    for j, half in enumerate(halves):
        part = jnp.dot(act[:, j * size : (j + 1) * size], half, preferred_element_type=jnp.float32)
        total = part if total is None else total + part
    return total


def to_gathered_order(act, rows):
    nx, nz, nc = [lax.axis_size(name) for name in REQ_PARTS]
    n = act.shape[0]
    own = lax.axis_index("c")
    split = act.reshape(n, nx, nz, nc, rows)
    split = jnp.where(own == 0, split, split[:, :, :, ::-1, :])
    return split.transpose(0, 3, 2, 1, 4).reshape(n, -1)


def per_device(
    queries,
    new_kv,
    cache_pool,
    page_table,
    assignment,
    lengths,
    lambda_vectors,
    subln_gain,
    residual,
    out_weight,
    norm_gain,
    gate_weight,
    up_weight,
    down_weight_t,
):
    widths = [out_weight.shape[1], gate_weight.shape[1], up_weight.shape[1], down_weight_t.shape[1]]
    packed = jnp.concatenate([out_weight, gate_weight, up_weight, down_weight_t], axis=1)
    rows_xz = gather_over_xz(packed)
    attn_out = attend(
        queries, new_kv, cache_pool, page_table, assignment, lengths, lambda_vectors, subln_gain
    )
    mlp_size = D // residual.shape[1]
    heads_all = mlp_gather(attn_out, mlp_size)
    rows_xz, heads_all = lax.optimization_barrier((rows_xz, heads_all))
    halves = swap_with_core(rows_xz)
    bounds = [0]
    for w in widths:
        bounds.append(bounds[-1] + w)
    out_full, gate_full, up_full, down_full = [
        [half[:, bounds[i] : bounds[i + 1]] for half in halves] for i in range(4)
    ]
    rows = out_weight.shape[0]
    projected = split_dot(to_gathered_order(heads_all, rows), out_full)
    stream = (residual.astype(jnp.float32) + projected).astype(jnp.bfloat16)
    stream_all = mlp_gather(stream, mlp_size).astype(jnp.float32)
    squares = jnp.sum(stream_all * stream_all, axis=1, keepdims=True)
    normed = (stream_all * lax.rsqrt(squares / D + 1e-05) * norm_gain).astype(jnp.bfloat16)
    normed = to_gathered_order(normed, rows)
    gate_up = split_dot(
        normed, [half[:, bounds[1] : bounds[3]] for half in halves]
    )
    gate_value = gate_up[:, : widths[1]]
    up_value = gate_up[:, widths[1] :]
    hidden_act = (jax.nn.silu(gate_value) * up_value).astype(jnp.bfloat16)
    summed = down_and_scatter(hidden_act, down_full, mlp_size, out_weight.shape[0])
    return (stream.astype(jnp.float32) + summed).astype(jnp.bfloat16)


def solution(mesh):
    split = Mesh(mesh.devices.reshape(4, 16, 2, mesh.devices.shape[1]), REQ_PARTS + ("mlp",))
    req = REQ_PARTS
    in_specs = (
        P(req, "mlp", None),
        P(req, "mlp", None),
        P(req, None, "mlp", None),
        P(req, None),
        P(req),
        P(),
        P(),
        P(),
        P(req, "mlp"),
        P(req, "mlp"),
        P(),
        P(req, "mlp"),
        P(req, "mlp"),
        P(req, "mlp"),
    )
    out_specs = P(req, "mlp")
    return jax.shard_map(
        per_device, mesh=split, in_specs=in_specs, out_specs=out_specs, check_vma=False
    )
```

```python
import jax
import jax.numpy as jnp
from jax import lax
from jax.sharding import Mesh, PartitionSpec as P

D = 2048


NEG_FILL = -1e30
LAMBDA_BASE = 0.2


def attend(
    queries, new_kv, cache_pool, page_table, assignment, lengths, lambda_vectors, subln_gain
):
    row_count, head_count, value_width = queries.shape
    half_size = value_width // 2
    score_scale = half_size ** (-0.5)
    request = assignment[0]
    cached = jnp.sum(
        jnp.where(jnp.arange(lengths.shape[0], dtype=jnp.int32) == request, lengths, 0)
    )
    pages = jnp.take(cache_pool, page_table[0], axis=0)
    cached_rows = pages.reshape(-1, head_count, cache_pool.shape[3])
    cache_len = cached_rows.shape[0]
    key_rows = jnp.concatenate([cached_rows, new_kv], axis=0)
    positions = jnp.arange(cache_len, dtype=jnp.int32)
    token_pos = jnp.arange(row_count, dtype=jnp.int32)
    visible = jnp.concatenate(
        [
            jnp.broadcast_to((positions < cached)[None, :], (row_count, cache_len)),
            token_pos[None, :] <= token_pos[:, None],
        ],
        axis=1,
    )
    value_rows = key_rows[:, :, 2 * half_size :]

    def one_map(query_rows, key_half):
        score = (
            jnp.einsum("nhd,khd->nhk", query_rows, key_half, preferred_element_type=jnp.float32)
            * score_scale
        )
        score = jnp.where(visible[:, None, :], score, NEG_FILL)
        row_max = jnp.max(score, axis=2, keepdims=True)
        exp_terms = jnp.where(visible[:, None, :], jnp.exp(score - row_max), 0.0)
        exp_total = jnp.sum(exp_terms, axis=2)
        mixed = jnp.einsum(
            "nhk,khd->nhd",
            exp_terms.astype(jnp.bfloat16),
            value_rows,
            preferred_element_type=jnp.float32,
        )
        return mixed / exp_total[:, :, None]

    map_one = one_map(queries[:, :, :half_size], key_rows[:, :, :half_size])
    map_two = one_map(queries[:, :, half_size:], key_rows[:, :, half_size : 2 * half_size])
    lambda_now = (
        jnp.exp(jnp.sum(lambda_vectors[0] * lambda_vectors[1]))
        - jnp.exp(jnp.sum(lambda_vectors[2] * lambda_vectors[3]))
        + LAMBDA_BASE
    )
    mix_out = map_one - lambda_now * map_two
    mix_out = (
        mix_out
        * lax.rsqrt(jnp.mean(mix_out * mix_out, axis=2, keepdims=True) + 1e-05)
        * subln_gain
        * (1.0 - LAMBDA_BASE)
    )
    return mix_out.astype(jnp.bfloat16).reshape(row_count, head_count * value_width)


def mlp_gather(block, axis_size):
    index = lax.axis_index("mlp")
    pieces = [block]
    for shift in range(1, axis_size):
        pieces.append(
            lax.ppermute(block, "mlp", [(i, (i + shift) % axis_size) for i in range(axis_size)])
        )
    slots = []
    for j in range(axis_size):
        chosen = pieces[0]
        for k in range(1, axis_size):
            chosen = jnp.where((index - k) % axis_size == j, pieces[k], chosen)
        slots.append(chosen)
    return jnp.concatenate(slots, axis=1)


def down_and_scatter(hidden_act, down_halves, axis_size, rows):
    index = lax.axis_index("mlp")
    nx, nz, nc = [lax.axis_size(name) for name in REQ_PARTS]
    n = hidden_act.shape[0]
    own = lax.axis_index("c")
    parts = []
    for half in down_halves:
        value = lax.dot_general(
            hidden_act, half, (((1,), (1,)), ((), ())), preferred_element_type=jnp.float32
        )
        parts.append(value.astype(jnp.bfloat16).reshape(n, nz, nx, rows))
    both = jnp.stack(parts, axis=1)
    both = jnp.where(own == 0, both, both[:, ::-1])

    def block_for(target):
        picked = lax.dynamic_index_in_dim(both, target, 3, keepdims=False)
        return picked.transpose(0, 2, 1, 3).reshape(n, -1)

    incoming = []
    for shift in range(1, axis_size):
        target = (index + shift) % axis_size
        incoming.append(
            lax.ppermute(
                block_for(target), "mlp", [(i, (i + shift) % axis_size) for i in range(axis_size)]
            )
        )
    total = block_for(index).astype(jnp.float32)
    for received in incoming:
        total = total + received.astype(jnp.float32)
    return total


REQ_PARTS = ("x", "z", "c")


def gather_over_xz(block):
    out = lax.all_gather(block, "x", axis=0, tiled=True)
    return lax.all_gather(out, "z", axis=0, tiled=True)


def swap_with_core(rows_xz):
    return [rows_xz, lax.ppermute(rows_xz, "c", [(0, 1), (1, 0)])]


def split_dot(act, halves):
    size = halves[0].shape[0]
    total = None
    for j, half in enumerate(halves):
        part = jnp.dot(act[:, j * size : (j + 1) * size], half, preferred_element_type=jnp.float32)
        total = part if total is None else total + part
    return total


def to_gathered_order(act, rows):
    nx, nz, nc = [lax.axis_size(name) for name in REQ_PARTS]
    n = act.shape[0]
    own = lax.axis_index("c")
    split = act.reshape(n, nx, nz, nc, rows)
    split = jnp.where(own == 0, split, split[:, :, :, ::-1, :])
    return split.transpose(0, 3, 2, 1, 4).reshape(n, -1)


def per_device(
    queries,
    new_kv,
    cache_pool,
    page_table,
    assignment,
    lengths,
    lambda_vectors,
    subln_gain,
    residual,
    out_weight,
    norm_gain,
    gate_weight,
    up_weight,
    down_weight_t,
):
    widths = [out_weight.shape[1], gate_weight.shape[1], up_weight.shape[1], down_weight_t.shape[1]]
    packed = jnp.concatenate([out_weight, gate_weight, up_weight, down_weight_t], axis=1)
    rows_xz = gather_over_xz(packed)
    attn_out = attend(
        queries, new_kv, cache_pool, page_table, assignment, lengths, lambda_vectors, subln_gain
    )
    mlp_size = D // residual.shape[1]
    heads_all = mlp_gather(attn_out, mlp_size)
    rows_xz, heads_all = lax.optimization_barrier((rows_xz, heads_all))
    halves = swap_with_core(rows_xz)
    bounds = [0]
    for w in widths:
        bounds.append(bounds[-1] + w)
    out_full, gate_full, up_full, down_full = [
        [half[:, bounds[i] : bounds[i + 1]] for half in halves] for i in range(4)
    ]
    rows = out_weight.shape[0]
    projected = split_dot(to_gathered_order(heads_all, rows), out_full)
    stream = (residual.astype(jnp.float32) + projected).astype(jnp.bfloat16)
    stream_all = mlp_gather(stream, mlp_size).astype(jnp.float32)
    squares = jnp.sum(stream_all * stream_all, axis=1, keepdims=True)
    normed = (stream_all * lax.rsqrt(squares / D + 1e-05) * norm_gain).astype(jnp.bfloat16)
    normed = to_gathered_order(normed, rows)
    gate_up = split_dot(
        normed, [half[:, bounds[1] : bounds[3]] for half in halves]
    )
    gate_value = gate_up[:, : widths[1]]
    up_value = gate_up[:, widths[1] :]
    hidden_act = (jax.nn.silu(gate_value) * up_value).astype(jnp.bfloat16)
    summed = down_and_scatter(hidden_act, down_full, mlp_size, out_weight.shape[0])
    return (stream.astype(jnp.float32) + summed).astype(jnp.bfloat16)


def solution(mesh):
    split = Mesh(mesh.devices.reshape(4, 16, 2, mesh.devices.shape[1]), REQ_PARTS + ("mlp",))
    req = REQ_PARTS
    in_specs = (
        P(req, "mlp", None),
        P(req, "mlp", None),
        P(req, None, "mlp", None),
        P(req, None),
        P(req),
        P(),
        P(),
        P(),
        P(req, "mlp"),
        P(req, "mlp"),
        P(),
        P(req, "mlp"),
        P(req, "mlp"),
        P(req, "mlp"),
    )
    out_specs = P(req, "mlp")
    return jax.shard_map(
        per_device, mesh=split, in_specs=in_specs, out_specs=out_specs, check_vma=False
    )
```

```python
import jax
import jax.numpy as jnp
from jax import lax
from jax.sharding import Mesh, PartitionSpec as P

D = 2048


NEG_FILL = -1e30
LAMBDA_BASE = 0.2


def attend(
    queries, new_kv, cache_pool, page_table, assignment, lengths, lambda_vectors, subln_gain
):
    row_count, head_count, value_width = queries.shape
    half_size = value_width // 2
    score_scale = half_size ** (-0.5)
    request = assignment[0]
    cached = jnp.sum(
        jnp.where(jnp.arange(lengths.shape[0], dtype=jnp.int32) == request, lengths, 0)
    )
    pages = jnp.take(cache_pool, page_table[0], axis=0)
    cached_rows = pages.reshape(-1, head_count, cache_pool.shape[3])
    cache_len = cached_rows.shape[0]
    key_rows = jnp.concatenate([cached_rows, new_kv], axis=0)
    positions = jnp.arange(cache_len, dtype=jnp.int32)
    token_pos = jnp.arange(row_count, dtype=jnp.int32)
    visible = jnp.concatenate(
        [
            jnp.broadcast_to((positions < cached)[None, :], (row_count, cache_len)),
            token_pos[None, :] <= token_pos[:, None],
        ],
        axis=1,
    )
    value_rows = key_rows[:, :, 2 * half_size :]

    def one_map(query_rows, key_half):
        score = (
            jnp.einsum("nhd,khd->nhk", query_rows, key_half, preferred_element_type=jnp.float32)
            * score_scale
        )
        score = jnp.where(visible[:, None, :], score, NEG_FILL)
        row_max = jnp.max(score, axis=2, keepdims=True)
        exp_terms = jnp.where(visible[:, None, :], jnp.exp(score - row_max), 0.0)
        exp_total = jnp.sum(exp_terms, axis=2)
        mixed = jnp.einsum(
            "nhk,khd->nhd",
            exp_terms.astype(jnp.bfloat16),
            value_rows,
            preferred_element_type=jnp.float32,
        )
        return mixed / exp_total[:, :, None]

    map_one = one_map(queries[:, :, :half_size], key_rows[:, :, :half_size])
    map_two = one_map(queries[:, :, half_size:], key_rows[:, :, half_size : 2 * half_size])
    lambda_now = (
        jnp.exp(jnp.sum(lambda_vectors[0] * lambda_vectors[1]))
        - jnp.exp(jnp.sum(lambda_vectors[2] * lambda_vectors[3]))
        + LAMBDA_BASE
    )
    mix_out = map_one - lambda_now * map_two
    mix_out = (
        mix_out
        * lax.rsqrt(jnp.mean(mix_out * mix_out, axis=2, keepdims=True) + 1e-05)
        * subln_gain
        * (1.0 - LAMBDA_BASE)
    )
    return mix_out.astype(jnp.bfloat16).reshape(row_count, head_count * value_width)


def mlp_gather(block, axis_size):
    index = lax.axis_index("mlp")
    pieces = [block]
    for shift in range(1, axis_size):
        pieces.append(
            lax.ppermute(block, "mlp", [(i, (i + shift) % axis_size) for i in range(axis_size)])
        )
    stacked = jnp.stack(pieces, axis=0)
    source_of = (index - jnp.arange(axis_size, dtype=jnp.int32)) % axis_size
    gathered = jnp.take(stacked, source_of, axis=0)
    return jnp.concatenate([gathered[k] for k in range(axis_size)], axis=1)


def down_and_scatter(hidden_act, down_halves, axis_size, rows):
    index = lax.axis_index("mlp")
    nx, nz, nc = [lax.axis_size(name) for name in REQ_PARTS]
    n = hidden_act.shape[0]
    own = lax.axis_index("c")
    parts = []
    for half in down_halves:
        value = lax.dot_general(
            hidden_act, half, (((1,), (1,)), ((), ())), preferred_element_type=jnp.float32
        )
        parts.append(value.astype(jnp.bfloat16).reshape(n, nz, nx, rows))
    both = jnp.stack(parts, axis=1)
    both = jnp.where(own == 0, both, both[:, ::-1])

    def block_for(target):
        picked = lax.dynamic_index_in_dim(both, target, 3, keepdims=False)
        return picked.transpose(0, 2, 1, 3).reshape(n, -1)

    incoming = []
    for shift in range(1, axis_size):
        target = (index + shift) % axis_size
        incoming.append(
            lax.ppermute(
                block_for(target), "mlp", [(i, (i + shift) % axis_size) for i in range(axis_size)]
            )
        )
    total = block_for(index).astype(jnp.float32)
    for received in incoming:
        total = total + received.astype(jnp.float32)
    return total


REQ_PARTS = ("x", "z", "c")


def gather_over_xz(block):
    out = lax.all_gather(block, "x", axis=0, tiled=True)
    return lax.all_gather(out, "z", axis=0, tiled=True)


def swap_with_core(rows_xz):
    return [rows_xz, lax.ppermute(rows_xz, "c", [(0, 1), (1, 0)])]


def split_dot(act, halves):
    size = halves[0].shape[0]
    total = None
    for j, half in enumerate(halves):
        part = jnp.dot(act[:, j * size : (j + 1) * size], half, preferred_element_type=jnp.float32)
        total = part if total is None else total + part
    return total


def to_gathered_order(act, rows):
    nx, nz, nc = [lax.axis_size(name) for name in REQ_PARTS]
    n = act.shape[0]
    own = lax.axis_index("c")
    split = act.reshape(n, nx, nz, nc, rows)
    split = jnp.where(own == 0, split, split[:, :, :, ::-1, :])
    return split.transpose(0, 3, 2, 1, 4).reshape(n, -1)


def per_device(
    queries,
    new_kv,
    cache_pool,
    page_table,
    assignment,
    lengths,
    lambda_vectors,
    subln_gain,
    residual,
    out_weight,
    norm_gain,
    gate_weight,
    up_weight,
    down_weight_t,
):
    widths = [out_weight.shape[1], gate_weight.shape[1], up_weight.shape[1], down_weight_t.shape[1]]
    packed = jnp.concatenate([out_weight, gate_weight, up_weight, down_weight_t], axis=1)
    rows_xz = gather_over_xz(packed)
    attn_out = attend(
        queries, new_kv, cache_pool, page_table, assignment, lengths, lambda_vectors, subln_gain
    )
    mlp_size = D // residual.shape[1]
    heads_all = mlp_gather(attn_out, mlp_size)
    rows_xz, heads_all = lax.optimization_barrier((rows_xz, heads_all))
    bounds = [0]
    for w in widths:
        bounds.append(bounds[-1] + w)
    out_full = swap_with_core(rows_xz[:, : bounds[1]])
    halves = swap_with_core(rows_xz[:, bounds[1] :])
    gate_full, up_full, down_full = [
        [half[:, bounds[i] - bounds[1] : bounds[i + 1] - bounds[1]] for half in halves]
        for i in range(1, 4)
    ]
    rows = out_weight.shape[0]
    projected = split_dot(to_gathered_order(heads_all, rows), out_full)
    stream = (residual.astype(jnp.float32) + projected).astype(jnp.bfloat16)
    stream_all = mlp_gather(stream, mlp_size).astype(jnp.float32)
    squares = jnp.sum(stream_all * stream_all, axis=1, keepdims=True)
    normed = (stream_all * lax.rsqrt(squares / D + 1e-05) * norm_gain).astype(jnp.bfloat16)
    normed = to_gathered_order(normed, rows)
    gate_up = split_dot(
        normed, [half[:, : bounds[3] - bounds[1]] for half in halves]
    )
    gate_value = gate_up[:, : widths[1]]
    up_value = gate_up[:, widths[1] :]
    hidden_act = (jax.nn.silu(gate_value) * up_value).astype(jnp.bfloat16)
    summed = down_and_scatter(hidden_act, down_full, mlp_size, out_weight.shape[0])
    return (stream.astype(jnp.float32) + summed).astype(jnp.bfloat16)


def solution(mesh):
    split = Mesh(mesh.devices.reshape(4, 16, 2, mesh.devices.shape[1]), REQ_PARTS + ("mlp",))
    req = REQ_PARTS
    in_specs = (
        P(req, "mlp", None),
        P(req, "mlp", None),
        P(req, None, "mlp", None),
        P(req, None),
        P(req),
        P(),
        P(),
        P(),
        P(req, "mlp"),
        P(req, "mlp"),
        P(),
        P(req, "mlp"),
        P(req, "mlp"),
        P(req, "mlp"),
    )
    out_specs = P(req, "mlp")
    return jax.shard_map(
        per_device, mesh=split, in_specs=in_specs, out_specs=out_specs, check_vma=False
    )
```

```python
import jax
import jax.numpy as jnp
from jax import lax
from jax.sharding import Mesh, PartitionSpec as P

D = 2048


NEG_FILL = -1e30
LAMBDA_BASE = 0.2


def attend(
    queries, new_kv, cache_pool, page_table, assignment, lengths, lambda_vectors, subln_gain
):
    row_count, head_count, value_width = queries.shape
    half_size = value_width // 2
    score_scale = half_size ** (-0.5)
    request = assignment[0]
    cached = jnp.sum(
        jnp.where(jnp.arange(lengths.shape[0], dtype=jnp.int32) == request, lengths, 0)
    )
    pages = jnp.take(cache_pool, page_table[0], axis=0)
    cached_rows = pages.reshape(-1, head_count, cache_pool.shape[3])
    cache_len = cached_rows.shape[0]
    key_rows = jnp.concatenate([cached_rows, new_kv], axis=0)
    positions = jnp.arange(cache_len, dtype=jnp.int32)
    token_pos = jnp.arange(row_count, dtype=jnp.int32)
    visible = jnp.concatenate(
        [
            jnp.broadcast_to((positions < cached)[None, :], (row_count, cache_len)),
            token_pos[None, :] <= token_pos[:, None],
        ],
        axis=1,
    )
    value_rows = key_rows[:, :, 2 * half_size :]

    def one_map(query_rows, key_half):
        score = (
            jnp.einsum("nhd,khd->nhk", query_rows, key_half, preferred_element_type=jnp.float32)
            * score_scale
        )
        score = jnp.where(visible[:, None, :], score, NEG_FILL)
        row_max = jnp.max(score, axis=2, keepdims=True)
        exp_terms = jnp.where(visible[:, None, :], jnp.exp(score - row_max), 0.0)
        exp_total = jnp.sum(exp_terms, axis=2)
        mixed = jnp.einsum(
            "nhk,khd->nhd",
            exp_terms.astype(jnp.bfloat16),
            value_rows,
            preferred_element_type=jnp.float32,
        )
        return mixed / exp_total[:, :, None]

    map_one = one_map(queries[:, :, :half_size], key_rows[:, :, :half_size])
    map_two = one_map(queries[:, :, half_size:], key_rows[:, :, half_size : 2 * half_size])
    lambda_now = (
        jnp.exp(jnp.sum(lambda_vectors[0] * lambda_vectors[1]))
        - jnp.exp(jnp.sum(lambda_vectors[2] * lambda_vectors[3]))
        + LAMBDA_BASE
    )
    mix_out = map_one - lambda_now * map_two
    mix_out = (
        mix_out
        * lax.rsqrt(jnp.mean(mix_out * mix_out, axis=2, keepdims=True) + 1e-05)
        * subln_gain
        * (1.0 - LAMBDA_BASE)
    )
    return mix_out.astype(jnp.bfloat16).reshape(row_count, head_count * value_width)


def mlp_gather(block, axis_size):
    index = lax.axis_index("mlp")
    pieces = [block]
    for shift in range(1, axis_size):
        pieces.append(
            lax.ppermute(block, "mlp", [(i, (i + shift) % axis_size) for i in range(axis_size)])
        )
    stacked = jnp.stack(pieces, axis=0)
    source_of = (index - jnp.arange(axis_size, dtype=jnp.int32)) % axis_size
    gathered = jnp.take(stacked, source_of, axis=0)
    return jnp.concatenate([gathered[k] for k in range(axis_size)], axis=1)


def down_and_scatter(hidden_act, down_halves, axis_size, rows):
    index = lax.axis_index("mlp")
    nx, nz, nc = [lax.axis_size(name) for name in REQ_PARTS]
    n = hidden_act.shape[0]
    own = lax.axis_index("c")
    parts = []
    for half in down_halves:
        value = lax.dot_general(
            hidden_act, half, (((1,), (1,)), ((), ())), preferred_element_type=jnp.float32
        )
        parts.append(value.astype(jnp.bfloat16).reshape(n, nz, nx, rows))

    def block_for(target):
        picks = [lax.dynamic_index_in_dim(p, target, 2, keepdims=False) for p in parts]
        first = jnp.where(own == 0, picks[0], picks[1])
        second = jnp.where(own == 0, picks[1], picks[0])
        return jnp.stack([first, second], axis=2).reshape(n, -1)

    incoming = []
    for shift in range(1, axis_size):
        target = (index + shift) % axis_size
        incoming.append(
            lax.ppermute(
                block_for(target), "mlp", [(i, (i + shift) % axis_size) for i in range(axis_size)]
            )
        )
    total = block_for(index).astype(jnp.float32)
    for received in incoming:
        total = total + received.astype(jnp.float32)
    return total


REQ_PARTS = ("x", "z", "c")


def gather_over_xz(block):
    out = lax.all_gather(block, "x", axis=0, tiled=True)
    return lax.all_gather(out, "z", axis=0, tiled=True)


def swap_with_core(rows_xz):
    return [rows_xz, lax.ppermute(rows_xz, "c", [(0, 1), (1, 0)])]


def split_dot(act, halves):
    size = halves[0].shape[0]
    total = None
    for j, half in enumerate(halves):
        part = jnp.dot(act[:, j * size : (j + 1) * size], half, preferred_element_type=jnp.float32)
        total = part if total is None else total + part
    return total


def to_gathered_order(act, rows):
    nx, nz, nc = [lax.axis_size(name) for name in REQ_PARTS]
    n = act.shape[0]
    own = lax.axis_index("c")
    split = act.reshape(n, nx, nz, nc, rows)
    split = jnp.where(own == 0, split, split[:, :, :, ::-1, :])
    return split.transpose(0, 3, 2, 1, 4).reshape(n, -1)


def per_device(
    queries,
    new_kv,
    cache_pool,
    page_table,
    assignment,
    lengths,
    lambda_vectors,
    subln_gain,
    residual,
    out_weight,
    norm_gain,
    gate_weight,
    up_weight,
    down_weight_t,
):
    widths = [out_weight.shape[1], gate_weight.shape[1], up_weight.shape[1], down_weight_t.shape[1]]
    packed = jnp.concatenate([out_weight, gate_weight, up_weight, down_weight_t], axis=1)
    rows_xz = gather_over_xz(packed)
    attn_out = attend(
        queries, new_kv, cache_pool, page_table, assignment, lengths, lambda_vectors, subln_gain
    )
    mlp_size = D // residual.shape[1]
    heads_all = mlp_gather(attn_out, mlp_size)
    rows_xz, heads_all = lax.optimization_barrier((rows_xz, heads_all))
    halves = swap_with_core(rows_xz)
    bounds = [0]
    for w in widths:
        bounds.append(bounds[-1] + w)
    out_full, gate_full, up_full, down_full = [
        [half[:, bounds[i] : bounds[i + 1]] for half in halves] for i in range(4)
    ]
    rows = out_weight.shape[0]
    projected = split_dot(to_gathered_order(heads_all, rows), out_full)
    stream = (residual.astype(jnp.float32) + projected).astype(jnp.bfloat16)
    stream_all = mlp_gather(stream, mlp_size).astype(jnp.float32)
    squares = jnp.sum(stream_all * stream_all, axis=1, keepdims=True)
    normed = (stream_all * lax.rsqrt(squares / D + 1e-05) * norm_gain).astype(jnp.bfloat16)
    normed = to_gathered_order(normed, rows)
    gate_up = split_dot(
        normed, [half[:, bounds[1] : bounds[3]] for half in halves]
    )
    gate_value = gate_up[:, : widths[1]]
    up_value = gate_up[:, widths[1] :]
    hidden_act = (jax.nn.silu(gate_value) * up_value).astype(jnp.bfloat16)
    summed = down_and_scatter(hidden_act, down_full, mlp_size, out_weight.shape[0])
    return (stream.astype(jnp.float32) + summed).astype(jnp.bfloat16)


def solution(mesh):
    split = Mesh(mesh.devices.reshape(4, 16, 2, mesh.devices.shape[1]), REQ_PARTS + ("mlp",))
    req = REQ_PARTS
    in_specs = (
        P(req, "mlp", None),
        P(req, "mlp", None),
        P(req, None, "mlp", None),
        P(req, None),
        P(req),
        P(),
        P(),
        P(),
        P(req, "mlp"),
        P(req, "mlp"),
        P(),
        P(req, "mlp"),
        P(req, "mlp"),
        P(req, "mlp"),
    )
    out_specs = P(req, "mlp")
    return jax.shard_map(
        per_device, mesh=split, in_specs=in_specs, out_specs=out_specs, check_vma=False
    )
```

```python
import jax
import jax.numpy as jnp
from jax import lax
from jax.sharding import Mesh, PartitionSpec as P

D = 2048


NEG_FILL = -1e30
LAMBDA_BASE = 0.2


def attend(
    queries, new_kv, cache_pool, page_table, assignment, lengths, lambda_vectors, subln_gain
):
    row_count, head_count, value_width = queries.shape
    half_size = value_width // 2
    score_scale = half_size ** (-0.5)
    request = assignment[0]
    cached = jnp.sum(
        jnp.where(jnp.arange(lengths.shape[0], dtype=jnp.int32) == request, lengths, 0)
    )
    pages = jnp.take(cache_pool, page_table[0], axis=0)
    cached_rows = pages.reshape(-1, head_count, cache_pool.shape[3])
    cache_len = cached_rows.shape[0]
    key_rows = jnp.concatenate([cached_rows, new_kv], axis=0)
    positions = jnp.arange(cache_len, dtype=jnp.int32)
    token_pos = jnp.arange(row_count, dtype=jnp.int32)
    visible = jnp.concatenate(
        [
            jnp.broadcast_to((positions < cached)[None, :], (row_count, cache_len)),
            token_pos[None, :] <= token_pos[:, None],
        ],
        axis=1,
    )
    value_rows = key_rows[:, :, 2 * half_size :]

    def one_map(query_rows, key_half):
        score = (
            jnp.einsum("nhd,khd->nhk", query_rows, key_half, preferred_element_type=jnp.float32)
            * score_scale
        )
        score = jnp.where(visible[:, None, :], score, NEG_FILL)
        row_max = jnp.max(score, axis=2, keepdims=True)
        exp_terms = jnp.where(visible[:, None, :], jnp.exp(score - row_max), 0.0)
        exp_total = jnp.sum(exp_terms, axis=2)
        mixed = jnp.einsum(
            "nhk,khd->nhd",
            exp_terms.astype(jnp.bfloat16),
            value_rows,
            preferred_element_type=jnp.float32,
        )
        return mixed / exp_total[:, :, None]

    map_one = one_map(queries[:, :, :half_size], key_rows[:, :, :half_size])
    map_two = one_map(queries[:, :, half_size:], key_rows[:, :, half_size : 2 * half_size])
    lambda_now = (
        jnp.exp(jnp.sum(lambda_vectors[0] * lambda_vectors[1]))
        - jnp.exp(jnp.sum(lambda_vectors[2] * lambda_vectors[3]))
        + LAMBDA_BASE
    )
    mix_out = map_one - lambda_now * map_two
    mix_out = (
        mix_out
        * lax.rsqrt(jnp.mean(mix_out * mix_out, axis=2, keepdims=True) + 1e-05)
        * subln_gain
        * (1.0 - LAMBDA_BASE)
    )
    return mix_out.astype(jnp.bfloat16).reshape(row_count, head_count * value_width)


def mlp_gather(block, axis_size):
    index = lax.axis_index("mlp")
    pieces = [block]
    for shift in range(1, axis_size):
        pieces.append(
            lax.ppermute(block, "mlp", [(i, (i + shift) % axis_size) for i in range(axis_size)])
        )
    ring = jnp.concatenate(pieces[::-1] + pieces[::-1], axis=1)
    width = block.shape[1]
    start = ((axis_size - 1 - index) % axis_size) * width
    return lax.dynamic_slice_in_dim(ring, start, axis_size * width, 1)


def down_and_scatter(hidden_act, down_halves, axis_size, rows):
    index = lax.axis_index("mlp")
    nx, nz, nc = [lax.axis_size(name) for name in REQ_PARTS]
    n = hidden_act.shape[0]
    own = lax.axis_index("c")
    parts = []
    for half in down_halves:
        value = lax.dot_general(
            hidden_act, half, (((1,), (1,)), ((), ())), preferred_element_type=jnp.float32
        )
        parts.append(value.astype(jnp.bfloat16).reshape(n, nz, nx, rows))

    def block_for(target):
        picks = [lax.dynamic_index_in_dim(p, target, 2, keepdims=False) for p in parts]
        first = jnp.where(own == 0, picks[0], picks[1])
        second = jnp.where(own == 0, picks[1], picks[0])
        return jnp.stack([first, second], axis=2).reshape(n, -1)

    incoming = []
    for shift in range(1, axis_size):
        target = (index + shift) % axis_size
        incoming.append(
            lax.ppermute(
                block_for(target), "mlp", [(i, (i + shift) % axis_size) for i in range(axis_size)]
            )
        )
    total = block_for(index).astype(jnp.float32)
    for received in incoming:
        total = total + received.astype(jnp.float32)
    return total


REQ_PARTS = ("x", "z", "c")


def gather_over_xz(block):
    out = lax.all_gather(block, "x", axis=0, tiled=True)
    return lax.all_gather(out, "z", axis=0, tiled=True)


def swap_with_core(rows_xz):
    return [rows_xz, lax.ppermute(rows_xz, "c", [(0, 1), (1, 0)])]


def split_dot(act, halves):
    size = halves[0].shape[0]
    total = None
    for j, half in enumerate(halves):
        part = jnp.dot(act[:, j * size : (j + 1) * size], half, preferred_element_type=jnp.float32)
        total = part if total is None else total + part
    return total


def to_gathered_order(act, rows):
    nx, nz, nc = [lax.axis_size(name) for name in REQ_PARTS]
    n = act.shape[0]
    own = lax.axis_index("c")
    split = act.reshape(n, nx, nz, nc, rows)
    split = jnp.where(own == 0, split, split[:, :, :, ::-1, :])
    return split.transpose(0, 3, 2, 1, 4).reshape(n, -1)


def per_device(
    queries,
    new_kv,
    cache_pool,
    page_table,
    assignment,
    lengths,
    lambda_vectors,
    subln_gain,
    residual,
    out_weight,
    norm_gain,
    gate_weight,
    up_weight,
    down_weight_t,
):
    widths = [out_weight.shape[1], gate_weight.shape[1], up_weight.shape[1], down_weight_t.shape[1]]
    packed = jnp.concatenate([out_weight, gate_weight, up_weight, down_weight_t], axis=1)
    rows_xz = gather_over_xz(packed)
    attn_out = attend(
        queries, new_kv, cache_pool, page_table, assignment, lengths, lambda_vectors, subln_gain
    )
    mlp_size = D // residual.shape[1]
    heads_all = mlp_gather(attn_out, mlp_size)
    rows_xz, heads_all = lax.optimization_barrier((rows_xz, heads_all))
    halves = swap_with_core(rows_xz)
    bounds = [0]
    for w in widths:
        bounds.append(bounds[-1] + w)
    out_full, gate_full, up_full, down_full = [
        [half[:, bounds[i] : bounds[i + 1]] for half in halves] for i in range(4)
    ]
    rows = out_weight.shape[0]
    projected = split_dot(to_gathered_order(heads_all, rows), out_full)
    stream = (residual.astype(jnp.float32) + projected).astype(jnp.bfloat16)
    stream_all = mlp_gather(stream, mlp_size).astype(jnp.float32)
    squares = jnp.sum(stream_all * stream_all, axis=1, keepdims=True)
    normed = (stream_all * lax.rsqrt(squares / D + 1e-05) * norm_gain).astype(jnp.bfloat16)
    normed = to_gathered_order(normed, rows)
    gate_up = split_dot(
        normed, [half[:, bounds[1] : bounds[3]] for half in halves]
    )
    gate_value = gate_up[:, : widths[1]]
    up_value = gate_up[:, widths[1] :]
    hidden_act = (jax.nn.silu(gate_value) * up_value).astype(jnp.bfloat16)
    summed = down_and_scatter(hidden_act, down_full, mlp_size, out_weight.shape[0])
    return (stream.astype(jnp.float32) + summed).astype(jnp.bfloat16)


def solution(mesh):
    split = Mesh(mesh.devices.reshape(4, 16, 2, mesh.devices.shape[1]), REQ_PARTS + ("mlp",))
    req = REQ_PARTS
    in_specs = (
        P(req, "mlp", None),
        P(req, "mlp", None),
        P(req, None, "mlp", None),
        P(req, None),
        P(req),
        P(),
        P(),
        P(),
        P(req, "mlp"),
        P(req, "mlp"),
        P(),
        P(req, "mlp"),
        P(req, "mlp"),
        P(req, "mlp"),
    )
    out_specs = P(req, "mlp")
    return jax.shard_map(
        per_device, mesh=split, in_specs=in_specs, out_specs=out_specs, check_vma=False
    )
```
